32 devices in a mesh: dp: 4 (over y, x), expert: 8 (over z, core).
Axes of the slice: x: 2, y: 2, z: 4, core: 2. Of those that a mesh axis runs over, the one named last changes fastest.
Arguments:
- tokens: bfloat16 [4096, 3584], P(('dp', 'expert')), may hold values from -6 to 6
- gate_probs: float32 [4096, 8], P(('dp', 'expert')), may hold values from 0.1 to 1
- expert_ids: int32 [4096, 8], P(('dp', 'expert')), may hold values from 0 to 63, all different within a row; in each aligned block of 128 rows (0 to 127, 128 to 255, ...) at most 24 rows name the same one
- cotangent: bfloat16 [4096, 3584], P(('dp', 'expert')), may hold values from -6 to 6
- w_gate: bfloat16 [8, 3584, 2048], P('expert', None, 'dp'), may hold values from -0.09375 to 0.09375
- w_up: bfloat16 [8, 3584, 2048], P('expert', None, 'dp'), may hold values from -0.09375 to 0.09375
- w_down: bfloat16 [8, 2048, 3584], P('expert', 'dp'), may hold values from -0.125 to 0.125
Outputs:
- layer_out: bfloat16 [4096, 3584], P(('dp', 'expert'))
- grad_tokens: bfloat16 [4096, 3584], P(('dp', 'expert'))
- grad_probs: float32 [4096, 8], P(('dp', 'expert'))
- grad_gate: bfloat16 [8, 3584, 2048], P('expert', None, 'dp')
- grad_up: bfloat16 [8, 3584, 2048], P('expert', None, 'dp')
- grad_down: bfloat16 [8, 2048, 3584], P('expert', 'dp')
The draws below stay inside these ranges and needn't reach their ends.
Inputs may be any that keep to these rules, and one draw needn't show every extreme that they name: `expert_ids`: each token names 8 distinct ids. Among the 128 tokens of one device no id is named by more than 24 of them, a bound that some block reaches. Only ids below 8 belong to the window.
All inputs are finite; a program needn't handle non-finite values.
Results may differ from the reference program's by a relative error of at most 0.012.
Values may be sent and summed in bfloat16 or wider, within the bound.
No kernel may reach another device: no remote copies, remote signals or barrier semaphores. Data moves between devices by JAX's collectives and lax.ppermute only.
A program may use at most 192 MiB of HBM per device.

```python
import math
import jax
import jax.numpy as jnp
import numpy as np
from jax import lax

D = 3584
FF_DEV = 512
TOP = 8
TOK_DEV = 128
FF = 2048
EXPERTS = 8
ALL_EXPERTS = 64
CAP = 24
TOKENS = 4096
N_DP = 4
DEVICES = 32


def level_of(stream_key, shape, split, smallest, largest):
    def one(position, parts):
        draws = jax.random.uniform(jax.random.fold_in(jax.random.fold_in(stream_key, 6), position), (parts,), jnp.float32, smallest / len(split), largest / len(split))
        return jnp.repeat(jnp.exp(draws), shape[position] // parts).reshape((-1,) + (1,) * (len(shape) - position - 1))

    level = one(*split[0])
    for cut in split[1:]:
        level = level * one(*cut)
    return level


def assign_block(key, own, number, rows, number_of, top, limit, slope):
    order = jax.random.permutation(key, number_of)
    packed, ordinary = shares(number_of, rows * top, limit, slope, True), shares(number_of, rows * top, limit, slope, False)
    places = jnp.arange(number_of)

    def named(lengths, rotation):
        used = int((lengths > 0).sum())
        fixed = max(1, used // 4)
        shifted = fixed + (places - fixed + rotation * (used - fixed)) % max(1, number_of - fixed)
        return jnp.zeros((number_of,), jnp.int32).at[order[jnp.where(places < fixed, places, shifted)]].set(jnp.asarray(lengths, jnp.int32))

    lengths = jnp.where(number % 4 == 0, named(packed, number // 4), named(ordinary, number - number // 4 - 1))
    mixed = jax.random.permutation(jax.random.fold_in(own, 3), number_of)
    source_of, taker = mixed[0:number_of // 2 * 2:2], mixed[1:number_of // 2 * 2:2]
    slack = jnp.minimum(lengths[source_of] - 1, limit - lengths[taker]) // 2
    slack = jnp.where((source_of == order[0]) | (taker == order[0]) | (lengths[taker] == 0), 0, jnp.maximum(slack, 0))
    shifted = jax.random.randint(jax.random.fold_in(own, 4), (number_of // 2,), 0, 1 << 20) % (slack + 1)
    lengths = lengths.at[source_of].add(-shifted).at[taker].add(shifted)
    items = jnp.searchsorted(jnp.cumsum(lengths), jnp.arange(rows * top), side="right").astype(jnp.int32)
    table = items.reshape(top, rows).T
    table = table[jax.random.permutation(jax.random.fold_in(own, 1), rows)]
    rotation = jax.random.randint(jax.random.fold_in(own, 2), (rows, 1), 0, top)
    return jnp.take_along_axis(table, (jnp.arange(top)[None, :] + rotation) % top, axis=1)


def shares(count, total, most, skew, full):
    weights = [(1 << 20) // math.isqrt(rank ** skew) + 1 for rank in range(1, count + 1)]
    largest = most if full else min(most, max(-(-total // count), total * weights[0] // sum(weights)))
    least = 1 if total - largest >= count - 1 else 0
    counts, surplus = [largest] + [least] * (count - 1), total - largest - least * (count - 1)
    while surplus > 0:
        movable = [i for i in range(1, count) if counts[i] < largest] or [i for i in range(1, count) if counts[i] < most]
        mass, remaining = sum([weights[i] for i in movable]), surplus
        for i in movable:
            more = min(most - counts[i], max(1, remaining * weights[i] // mass), surplus)
            counts[i] = counts[i] + more
            surplus = surplus - more
    return np.array(counts)


def noise(stream_key, dims, deviation, bound, shards=(), held_as=jnp.bfloat16):
    drawn = deviation * jax.random.normal(stream_key, dims, jnp.float32)
    if shards:
        drawn = drawn * level_of(stream_key, dims, shards, -0.22, 0.18)
    return jnp.clip(drawn, -bound, bound).astype(held_as)


def setup_inputs(seed: int = 0) -> dict:
    arg_keys = jax.random.split(jax.random.key(seed), 8)
    tokens = noise(arg_keys[0], (TOKENS, D), 1.0, 6.0, ((0, 32),))
    gate_probs = jnp.clip(0.1 + 0.9 * jax.random.uniform(arg_keys[1], (TOKENS, TOP), jnp.float32) ** level_of(arg_keys[1], (TOKENS, TOP), ((0, 32),), -0.2, 0.2), 0.1, 1.0)
    expert_ids_keys = jax.random.split(jax.random.fold_in(arg_keys[2], 1), TOKENS // TOK_DEV)
    expert_ids_turns = jax.random.permutation(jax.random.fold_in(arg_keys[2], 3), TOKENS // TOK_DEV)
    expert_ids = jax.vmap(lambda own, number: assign_block(jax.random.fold_in(arg_keys[2], 2), own, number, TOK_DEV, ALL_EXPERTS, TOP, CAP, 2))(expert_ids_keys, expert_ids_turns).reshape((TOKENS, TOP))
    cotangent = noise(arg_keys[3], (TOKENS, D), 1.0, 6.0, ((0, 32),))
    w_gate = noise(arg_keys[4], (EXPERTS, D, FF), D ** -0.5, 0.09375, ((0, 8), (2, 4)))
    w_up = noise(arg_keys[5], (EXPERTS, D, FF), D ** -0.5, 0.09375, ((0, 8), (2, 4)))
    w_down = noise(arg_keys[6], (EXPERTS, FF, D), FF ** -0.5, 0.125, ((0, 8), (1, 4)))
    return {"tokens": tokens, "gate_probs": gate_probs, "expert_ids": expert_ids, "cotangent": cotangent, "w_gate": w_gate, "w_up": w_up, "w_down": w_down}


def device_table(dev_ids):
    flat_ids = dev_ids.reshape(-1).astype(jnp.int32)
    matches = (flat_ids[:, None] == jnp.arange(EXPERTS, dtype=jnp.int32)[None, :]).astype(jnp.int32)
    earlier = jnp.cumsum(matches, axis=0) - matches
    slot_pos = jnp.sum(earlier * matches, axis=1).astype(jnp.int32)
    target = jnp.where(flat_ids < EXPERTS, flat_ids * CAP + slot_pos, EXPERTS * CAP).astype(jnp.int32)
    flat_index = jnp.arange(TOK_DEV * TOP, dtype=jnp.int32)
    blank_table = jnp.full((EXPERTS * CAP,), TOK_DEV * TOP, jnp.int32)
    return blank_table.at[target].set(flat_index, mode="drop")


def reference(tokens, gate_probs, expert_ids, cotangent, w_gate, w_up, w_down):
    dev_ids = expert_ids.reshape(DEVICES, TOK_DEV * TOP)
    local_slots = jax.vmap(device_table)(dev_ids)
    offsets = (jnp.arange(DEVICES, dtype=jnp.int32) * (TOK_DEV * TOP))[:, None]
    global_slots = jnp.where(local_slots < TOK_DEV * TOP, local_slots + offsets, TOKENS * TOP).astype(jnp.int32)
    by_expert = jnp.transpose(global_slots.reshape(DEVICES, EXPERTS, CAP), (1, 0, 2)).reshape(EXPERTS, DEVICES * CAP)
    zero_row = jnp.zeros((1, D), tokens.dtype)
    padded_x = jnp.concatenate([tokens, zero_row], 0)
    padded_dy = jnp.concatenate([cotangent, zero_row], 0)
    padded_p = jnp.concatenate([gate_probs.reshape(-1), jnp.zeros((1,), gate_probs.dtype)], 0)
    row_count = DEVICES * CAP

    def expert_step(running, inputs):
        out_acc, dx_acc, score_acc = running
        gate_w, up_w, down_w, flat_slots = inputs
        token_of = (flat_slots // TOP).astype(jnp.int32)
        rows_x = padded_x[token_of]
        rows_dy = padded_dy[token_of]
        prob_rows = padded_p[flat_slots]
        rows_c = (prob_rows[:, None] * rows_dy.astype(jnp.float32)).astype(jnp.bfloat16)
        gate_pre = jnp.dot(rows_x, gate_w, preferred_element_type=jnp.float32)
        up_pre = jnp.dot(rows_x, up_w, preferred_element_type=jnp.float32)
        sigmoid_g = jax.nn.sigmoid(gate_pre)
        activated = gate_pre * sigmoid_g
        hidden = (activated * up_pre).astype(jnp.bfloat16)
        grad_hidden = jnp.dot(rows_c, down_w.T, preferred_element_type=jnp.float32)
        grad_upin = (grad_hidden * activated).astype(jnp.bfloat16)
        grad_gatein = (grad_hidden * up_pre * sigmoid_g * (1.0 + gate_pre * (1.0 - sigmoid_g))).astype(jnp.bfloat16)
        expert_out = jnp.zeros((row_count, D), jnp.float32)
        dx_rows = jnp.zeros((row_count, D), jnp.float32)
        for quarter in range(N_DP):
            lower = quarter * FF_DEV
            upper = lower + FF_DEV
            part_out = jnp.dot(hidden[:, lower:upper], down_w[lower:upper, :], preferred_element_type=jnp.float32)
            expert_out = expert_out + part_out.astype(jnp.bfloat16).astype(jnp.float32)
            part_dx = jnp.dot(grad_gatein[:, lower:upper], gate_w[:, lower:upper].T, preferred_element_type=jnp.float32)
            part_dx = part_dx + jnp.dot(grad_upin[:, lower:upper], up_w[:, lower:upper].T, preferred_element_type=jnp.float32)
            dx_rows = dx_rows + part_dx.astype(jnp.bfloat16).astype(jnp.float32)
        out_acc = out_acc.at[token_of].add(prob_rows[:, None] * expert_out)
        dx_acc = dx_acc.at[token_of].add(dx_rows)
        score_rows = jnp.sum(rows_dy.astype(jnp.float32) * expert_out, axis=1)
        score_acc = score_acc.at[flat_slots].set(score_rows)
        new_gate = jnp.dot(rows_x.T, grad_gatein, preferred_element_type=jnp.float32).astype(jnp.bfloat16)
        new_up = jnp.dot(rows_x.T, grad_upin, preferred_element_type=jnp.float32).astype(jnp.bfloat16)
        new_down = jnp.dot(hidden.T, rows_c, preferred_element_type=jnp.float32).astype(jnp.bfloat16)
        return (out_acc, dx_acc, score_acc), (new_gate, new_up, new_down)

    start = (jnp.zeros((TOKENS + 1, D), jnp.float32), jnp.zeros((TOKENS + 1, D), jnp.float32), jnp.zeros((TOKENS * TOP + 1,), jnp.float32))
    finals, grads = lax.scan(expert_step, start, (w_gate, w_up, w_down, by_expert))
    out_acc, dx_acc, score_acc = finals
    layer_out = out_acc[:TOKENS].astype(jnp.bfloat16)
    grad_tokens = dx_acc[:TOKENS].astype(jnp.bfloat16)
    grad_probs = score_acc[:TOKENS * TOP].reshape(TOKENS, TOP)
    return (layer_out, grad_tokens, grad_probs, grads[0], grads[1], grads[2])
```

```python
import jax
import jax.numpy as jnp
from jax import lax
from jax.sharding import PartitionSpec as P


def slot_table(flat_ids, experts, capacity, sentinel):
    matches = (flat_ids[:, None] == jnp.arange(experts, dtype=jnp.int32)[None, :]).astype(jnp.int32)
    earlier = jnp.cumsum(matches, axis=0) - matches
    slot_pos = jnp.sum(earlier * matches, axis=1)
    target = jnp.where(flat_ids < experts, flat_ids * capacity + slot_pos, experts * capacity)
    flat_index = jnp.arange(flat_ids.shape[0], dtype=jnp.int32)
    blank_table = jnp.full((experts * capacity,), sentinel, jnp.int32)
    return blank_table.at[target].set(flat_index, mode="drop")


def contract_last(left, right):
    return lax.dot_general(
        left, right, (((1,), (1,)), ((), ())), preferred_element_type=jnp.float32
    )


def contract_first(left, right):
    return lax.dot_general(
        left, right, (((0,), (0,)), ((), ())), preferred_element_type=jnp.float32
    )


def dispatch(send_rows):
    along_expert = lax.all_to_all(send_rows, "expert", split_axis=0, concat_axis=0, tiled=True)
    return lax.all_gather(along_expert, "dp", axis=0, tiled=True)


def gather_back(partial_rows, groups):
    by_group = lax.all_to_all(partial_rows, "dp", split_axis=0, concat_axis=0, tiled=True)
    rows = by_group.shape[0] // groups
    summed = jnp.sum(by_group.astype(jnp.float32).reshape(groups, rows, -1), axis=0)
    return lax.all_to_all(
        summed.astype(jnp.bfloat16), "expert", split_axis=0, concat_axis=0, tiled=True
    )


def on_device(tokens, gate_probs, expert_ids, cotangent, w_gate, w_up, w_down):
    tok_count, model_width = tokens.shape
    top_k = expert_ids.shape[1]
    experts = lax.axis_size("expert")
    groups = lax.axis_size("dp")
    capacity = 3 * tok_count * top_k // (16 * experts)
    flat_count = tok_count * top_k
    slots = slot_table(expert_ids.reshape(-1), experts, capacity, flat_count)
    token_of = slots // top_k
    zero_row = jnp.zeros((1, model_width), jnp.bfloat16)
    send_x = jnp.concatenate([tokens, zero_row], 0)[token_of]
    rows_dy = jnp.concatenate([cotangent, zero_row], 0)[token_of]
    prob_rows = jnp.concatenate([gate_probs.reshape(-1), jnp.zeros((1,), jnp.float32)], 0)[slots]
    send_c = (prob_rows[:, None] * rows_dy.astype(jnp.float32)).astype(jnp.bfloat16)
    rows_x = dispatch(send_x)
    rows_c = dispatch(send_c)
    gate_w = w_gate[0]
    up_w = w_up[0]
    down_w = w_down[0]
    gate_pre = jnp.dot(rows_x, gate_w, preferred_element_type=jnp.float32)
    up_pre = jnp.dot(rows_x, up_w, preferred_element_type=jnp.float32)
    sigmoid_g = jax.nn.sigmoid(gate_pre)
    activated = gate_pre * sigmoid_g
    hidden = (activated * up_pre).astype(jnp.bfloat16)
    part_out = jnp.dot(hidden, down_w, preferred_element_type=jnp.float32).astype(jnp.bfloat16)
    out_rows = gather_back(part_out, groups).astype(jnp.float32)
    grad_hidden = contract_last(rows_c, down_w)
    grad_upin = (grad_hidden * activated).astype(jnp.bfloat16)
    grad_gatein = (grad_hidden * up_pre * sigmoid_g * (1.0 + gate_pre * (1.0 - sigmoid_g))).astype(
        jnp.bfloat16
    )
    part_dx = (contract_last(grad_gatein, gate_w) + contract_last(grad_upin, up_w)).astype(
        jnp.bfloat16
    )
    dx_rows = gather_back(part_dx, groups).astype(jnp.float32)
    new_gate = contract_first(rows_x, grad_gatein).astype(jnp.bfloat16)[None]
    new_up = contract_first(rows_x, grad_upin).astype(jnp.bfloat16)[None]
    new_down = contract_first(hidden, rows_c).astype(jnp.bfloat16)[None]
    owner = (token_of[None, :] == jnp.arange(tok_count, dtype=jnp.int32)[:, None]).astype(
        jnp.float32
    )
    layer_out = jnp.dot(
        owner * prob_rows[None, :],
        out_rows,
        precision=lax.Precision.HIGHEST,
        preferred_element_type=jnp.float32,
    ).astype(jnp.bfloat16)
    grad_tokens = jnp.dot(
        owner, dx_rows, precision=lax.Precision.HIGHEST, preferred_element_type=jnp.float32
    ).astype(jnp.bfloat16)
    score_rows = jnp.sum(rows_dy.astype(jnp.float32) * out_rows, axis=1)
    grad_probs = (
        jnp.zeros((flat_count + 1,), jnp.float32)
        .at[slots]
        .set(score_rows)[:flat_count]
        .reshape(tok_count, top_k)
    )
    return (layer_out, grad_tokens, grad_probs, new_gate, new_up, new_down)


def solution(mesh):
    return jax.shard_map(
        on_device,
        mesh=mesh,
        in_specs=(
            P(("dp", "expert"), None),
            P(("dp", "expert"), None),
            P(("dp", "expert"), None),
            P(("dp", "expert"), None),
            P("expert", None, "dp"),
            P("expert", None, "dp"),
            P("expert", "dp", None),
        ),
        out_specs=(
            P(("dp", "expert"), None),
            P(("dp", "expert"), None),
            P(("dp", "expert"), None),
            P("expert", None, "dp"),
            P("expert", None, "dp"),
            P("expert", "dp", None),
        ),
        check_vma=False,
    )
```

```python
import jax
import jax.numpy as jnp
from jax import lax
from jax.sharding import PartitionSpec as P


def slot_table(flat_ids, experts, capacity, sentinel):
    matches = (flat_ids[:, None] == jnp.arange(experts, dtype=jnp.int32)[None, :]).astype(jnp.int32)
    earlier = jnp.cumsum(matches, axis=0) - matches
    slot_pos = jnp.sum(earlier * matches, axis=1)
    target = jnp.where(flat_ids < experts, flat_ids * capacity + slot_pos, experts * capacity)
    flat_index = jnp.arange(flat_ids.shape[0], dtype=jnp.int32)
    blank_table = jnp.full((experts * capacity,), sentinel, jnp.int32)
    return blank_table.at[target].set(flat_index, mode="drop")


def contract_last(left, right):
    return lax.dot_general(
        left, right, (((1,), (1,)), ((), ())), preferred_element_type=jnp.float32
    )


def contract_first(left, right):
    return lax.dot_general(
        left, right, (((0,), (0,)), ((), ())), preferred_element_type=jnp.float32
    )


def dispatch(send_rows):
    along_expert = lax.all_to_all(send_rows, "expert", split_axis=0, concat_axis=0, tiled=True)
    return lax.all_gather(along_expert, "dp", axis=0, tiled=True)


def gather_back(partial_rows, groups):
    summed = lax.psum_scatter(partial_rows, "dp", scatter_dimension=0, tiled=True)
    return lax.all_to_all(summed, "expert", split_axis=0, concat_axis=0, tiled=True)


def on_device(tokens, gate_probs, expert_ids, cotangent, w_gate, w_up, w_down):
    tok_count, model_width = tokens.shape
    top_k = expert_ids.shape[1]
    experts = lax.axis_size("expert")
    groups = lax.axis_size("dp")
    capacity = 3 * tok_count * top_k // (16 * experts)
    flat_count = tok_count * top_k
    slots = slot_table(expert_ids.reshape(-1), experts, capacity, flat_count)
    token_of = slots // top_k
    zero_row = jnp.zeros((1, model_width), jnp.bfloat16)
    send_x = jnp.concatenate([tokens, zero_row], 0)[token_of]
    rows_dy = jnp.concatenate([cotangent, zero_row], 0)[token_of]
    prob_rows = jnp.concatenate([gate_probs.reshape(-1), jnp.zeros((1,), jnp.float32)], 0)[slots]
    send_c = (prob_rows[:, None] * rows_dy.astype(jnp.float32)).astype(jnp.bfloat16)
    rows_x = dispatch(send_x)
    rows_c = dispatch(send_c)
    gate_w = w_gate[0]
    up_w = w_up[0]
    down_w = w_down[0]
    gate_pre = jnp.dot(rows_x, gate_w, preferred_element_type=jnp.float32)
    up_pre = jnp.dot(rows_x, up_w, preferred_element_type=jnp.float32)
    sigmoid_g = jax.nn.sigmoid(gate_pre)
    activated = gate_pre * sigmoid_g
    hidden = (activated * up_pre).astype(jnp.bfloat16)
    part_out = jnp.dot(hidden, down_w, preferred_element_type=jnp.float32).astype(jnp.bfloat16)
    out_rows = gather_back(part_out, groups).astype(jnp.float32)
    grad_hidden = contract_last(rows_c, down_w)
    grad_upin = (grad_hidden * activated).astype(jnp.bfloat16)
    grad_gatein = (grad_hidden * up_pre * sigmoid_g * (1.0 + gate_pre * (1.0 - sigmoid_g))).astype(
        jnp.bfloat16
    )
    part_dx = (contract_last(grad_gatein, gate_w) + contract_last(grad_upin, up_w)).astype(
        jnp.bfloat16
    )
    dx_rows = gather_back(part_dx, groups).astype(jnp.float32)
    new_gate = contract_first(rows_x, grad_gatein).astype(jnp.bfloat16)[None]
    new_up = contract_first(rows_x, grad_upin).astype(jnp.bfloat16)[None]
    new_down = contract_first(hidden, rows_c).astype(jnp.bfloat16)[None]
    owner = (token_of[None, :] == jnp.arange(tok_count, dtype=jnp.int32)[:, None]).astype(
        jnp.float32
    )
    layer_out = jnp.dot(
        owner * prob_rows[None, :],
        out_rows,
        precision=lax.Precision.HIGHEST,
        preferred_element_type=jnp.float32,
    ).astype(jnp.bfloat16)
    grad_tokens = jnp.dot(
        owner, dx_rows, precision=lax.Precision.HIGHEST, preferred_element_type=jnp.float32
    ).astype(jnp.bfloat16)
    score_rows = jnp.sum(rows_dy.astype(jnp.float32) * out_rows, axis=1)
    grad_probs = (
        jnp.zeros((flat_count + 1,), jnp.float32)
        .at[slots]
        .set(score_rows)[:flat_count]
        .reshape(tok_count, top_k)
    )
    return (layer_out, grad_tokens, grad_probs, new_gate, new_up, new_down)


def solution(mesh):
    return jax.shard_map(
        on_device,
        mesh=mesh,
        in_specs=(
            P(("dp", "expert"), None),
            P(("dp", "expert"), None),
            P(("dp", "expert"), None),
            P(("dp", "expert"), None),
            P("expert", None, "dp"),
            P("expert", None, "dp"),
            P("expert", "dp", None),
        ),
        out_specs=(
            P(("dp", "expert"), None),
            P(("dp", "expert"), None),
            P(("dp", "expert"), None),
            P("expert", None, "dp"),
            P("expert", None, "dp"),
            P("expert", "dp", None),
        ),
        check_vma=False,
    )
```

```python
import jax
import jax.numpy as jnp
from jax import lax
from jax.sharding import PartitionSpec as P


def slot_table(flat_ids, experts, capacity, sentinel):
    matches = (flat_ids[:, None] == jnp.arange(experts, dtype=jnp.int32)[None, :]).astype(jnp.int32)
    earlier = jnp.cumsum(matches, axis=0) - matches
    slot_pos = jnp.sum(earlier * matches, axis=1)
    target = jnp.where(flat_ids < experts, flat_ids * capacity + slot_pos, experts * capacity)
    flat_index = jnp.arange(flat_ids.shape[0], dtype=jnp.int32)
    blank_table = jnp.full((experts * capacity,), sentinel, jnp.int32)
    return blank_table.at[target].set(flat_index, mode="drop")


def contract_last(left, right):
    return lax.dot_general(
        left, right, (((1,), (1,)), ((), ())), preferred_element_type=jnp.float32
    )


def contract_first(left, right):
    return lax.dot_general(
        left, right, (((0,), (0,)), ((), ())), preferred_element_type=jnp.float32
    )


def dispatch(send_rows):
    along_expert = lax.all_to_all(send_rows, "expert", split_axis=0, concat_axis=0, tiled=True)
    return lax.all_gather(along_expert, "dp", axis=0, tiled=True)


def gather_back(partial_rows, groups):
    summed = lax.psum_scatter(partial_rows, "dp", scatter_dimension=0, tiled=True)
    return lax.all_to_all(summed, "expert", split_axis=0, concat_axis=0, tiled=True)


def expert_forward(rows_x, gate_w, up_w, down_w):
    gate_pre = jnp.dot(rows_x, gate_w, preferred_element_type=jnp.float32)
    up_pre = jnp.dot(rows_x, up_w, preferred_element_type=jnp.float32)
    hidden = (gate_pre * jax.nn.sigmoid(gate_pre) * up_pre).astype(jnp.bfloat16)
    part_out = jnp.dot(hidden, down_w, preferred_element_type=jnp.float32).astype(jnp.bfloat16)
    return lax.optimization_barrier((part_out, hidden, gate_pre, up_pre))


def expert_backward(rows_c, gate_pre, up_pre, gate_w, up_w, down_w):
    sigmoid_g = jax.nn.sigmoid(gate_pre)
    activated = gate_pre * sigmoid_g
    grad_hidden = contract_last(rows_c, down_w)
    grad_upin = (grad_hidden * activated).astype(jnp.bfloat16)
    grad_gatein = (grad_hidden * up_pre * sigmoid_g * (1.0 + gate_pre * (1.0 - sigmoid_g))).astype(
        jnp.bfloat16
    )
    part_dx = (contract_last(grad_gatein, gate_w) + contract_last(grad_upin, up_w)).astype(
        jnp.bfloat16
    )
    return part_dx, grad_gatein, grad_upin


def join_slots(chunks, experts, model_width):
    parts = [chunk.reshape(experts, -1, model_width) for chunk in chunks]
    return jnp.concatenate(parts, axis=1).reshape(-1, model_width)


def on_device(tokens, gate_probs, expert_ids, cotangent, w_gate, w_up, w_down):
    tok_count, model_width = tokens.shape
    top_k = expert_ids.shape[1]
    experts = lax.axis_size("expert")
    groups = lax.axis_size("dp")
    capacity = 3 * tok_count * top_k // (16 * experts)
    flat_count = tok_count * top_k
    slots = slot_table(expert_ids.reshape(-1), experts, capacity, flat_count)
    token_of = slots // top_k
    zero_row = jnp.zeros((1, model_width), jnp.bfloat16)
    send_x = jnp.concatenate([tokens, zero_row], 0)[token_of]
    rows_dy = jnp.concatenate([cotangent, zero_row], 0)[token_of]
    prob_rows = jnp.concatenate([gate_probs.reshape(-1), jnp.zeros((1,), jnp.float32)], 0)[slots]
    send_c = (prob_rows[:, None] * rows_dy.astype(jnp.float32)).astype(jnp.bfloat16)
    half = max(capacity // 2, 1)
    bounds = [(lo, hi) for lo, hi in ((0, half), (half, capacity)) if hi > lo]
    x_by_slot = send_x.reshape(experts, capacity, model_width)
    c_by_slot = send_c.reshape(experts, capacity, model_width)
    xs = [dispatch(x_by_slot[:, lo:hi].reshape(-1, model_width)) for lo, hi in bounds]
    cs = [dispatch(c_by_slot[:, lo:hi].reshape(-1, model_width)) for lo, hi in bounds]
    gate_w = w_gate[0]
    up_w = w_up[0]
    down_w = w_down[0]
    forwards = [expert_forward(rows_x, gate_w, up_w, down_w) for rows_x in xs]
    outs = [gather_back(fw[0], groups) for fw in forwards]
    backwards = [
        expert_backward(rows_c, fw[2], fw[3], gate_w, up_w, down_w)
        for rows_c, fw in zip(cs, forwards)
    ]
    dxs = [gather_back(bw[0], groups) for bw in backwards]
    new_gate = sum(contract_first(rx, bw[1]) for rx, bw in zip(xs, backwards))
    new_up = sum(contract_first(rx, bw[2]) for rx, bw in zip(xs, backwards))
    new_down = sum(contract_first(fw[1], rc) for fw, rc in zip(forwards, cs))
    new_gate = new_gate.astype(jnp.bfloat16)[None]
    new_up = new_up.astype(jnp.bfloat16)[None]
    new_down = new_down.astype(jnp.bfloat16)[None]
    out_rows = join_slots(outs, experts, model_width).astype(jnp.float32)
    dx_rows = join_slots(dxs, experts, model_width).astype(jnp.float32)
    owner = (token_of[None, :] == jnp.arange(tok_count, dtype=jnp.int32)[:, None]).astype(
        jnp.float32
    )
    layer_out = jnp.dot(
        owner * prob_rows[None, :],
        out_rows,
        precision=lax.Precision.HIGHEST,
        preferred_element_type=jnp.float32,
    ).astype(jnp.bfloat16)
    grad_tokens = jnp.dot(
        owner, dx_rows, precision=lax.Precision.HIGHEST, preferred_element_type=jnp.float32
    ).astype(jnp.bfloat16)
    score_rows = jnp.sum(rows_dy.astype(jnp.float32) * out_rows, axis=1)
    grad_probs = (
        jnp.zeros((flat_count + 1,), jnp.float32)
        .at[slots]
        .set(score_rows)[:flat_count]
        .reshape(tok_count, top_k)
    )
    return (layer_out, grad_tokens, grad_probs, new_gate, new_up, new_down)


def solution(mesh):
    return jax.shard_map(
        on_device,
        mesh=mesh,
        in_specs=(
            P(("dp", "expert"), None),
            P(("dp", "expert"), None),
            P(("dp", "expert"), None),
            P(("dp", "expert"), None),
            P("expert", None, "dp"),
            P("expert", None, "dp"),
            P("expert", "dp", None),
        ),
        out_specs=(
            P(("dp", "expert"), None),
            P(("dp", "expert"), None),
            P(("dp", "expert"), None),
            P("expert", None, "dp"),
            P("expert", None, "dp"),
            P("expert", "dp", None),
        ),
        check_vma=False,
    )
```

```python
import jax
import jax.numpy as jnp
from jax import lax
from jax.sharding import PartitionSpec as P


def slot_table(flat_ids, experts, capacity, sentinel):
    matches = (flat_ids[:, None] == jnp.arange(experts, dtype=jnp.int32)[None, :]).astype(jnp.int32)
    earlier = jnp.cumsum(matches, axis=0) - matches
    slot_pos = jnp.sum(earlier * matches, axis=1)
    target = jnp.where(flat_ids < experts, flat_ids * capacity + slot_pos, experts * capacity)
    flat_index = jnp.arange(flat_ids.shape[0], dtype=jnp.int32)
    blank_table = jnp.full((experts * capacity,), sentinel, jnp.int32)
    return blank_table.at[target].set(flat_index, mode="drop")


def contract_last(left, right):
    return lax.dot_general(
        left, right, (((1,), (1,)), ((), ())), preferred_element_type=jnp.float32
    )


def contract_first(left, right):
    return lax.dot_general(
        left, right, (((0,), (0,)), ((), ())), preferred_element_type=jnp.float32
    )


def along_expert(send_rows):
    return lax.all_to_all(send_rows, "expert", split_axis=0, concat_axis=0, tiled=True)


def gather_back(partial_rows, groups):
    summed = lax.psum_scatter(partial_rows, "dp", scatter_dimension=0, tiled=True)
    return lax.all_to_all(summed, "expert", split_axis=0, concat_axis=0, tiled=True)


def on_device(tokens, gate_probs, expert_ids, cotangent, w_gate, w_up, w_down):
    tok_count, model_width = tokens.shape
    top_k = expert_ids.shape[1]
    experts = lax.axis_size("expert")
    groups = lax.axis_size("dp")
    capacity = 3 * tok_count * top_k // (16 * experts)
    flat_count = tok_count * top_k
    slots = slot_table(expert_ids.reshape(-1), experts, capacity, flat_count)
    token_of = slots // top_k
    zero_row = jnp.zeros((1, model_width), jnp.bfloat16)
    send_x = jnp.concatenate([tokens, zero_row], 0)[token_of]
    rows_dy = jnp.concatenate([cotangent, zero_row], 0)[token_of]
    prob_rows = jnp.concatenate([gate_probs.reshape(-1), jnp.zeros((1,), jnp.float32)], 0)[slots]
    send_c = (prob_rows[:, None] * rows_dy.astype(jnp.float32)).astype(jnp.bfloat16)
    rows_x = lax.all_gather(along_expert(send_x), "dp", axis=0, tiled=True)
    rows_x, c_along = lax.optimization_barrier((rows_x, along_expert(send_c)))
    rows_c = lax.all_gather(c_along, "dp", axis=0, tiled=True)
    gate_w = w_gate[0]
    up_w = w_up[0]
    down_w = w_down[0]
    gate_pre = jnp.dot(rows_x, gate_w, preferred_element_type=jnp.float32)
    up_pre = jnp.dot(rows_x, up_w, preferred_element_type=jnp.float32)
    sigmoid_g = jax.nn.sigmoid(gate_pre)
    activated = gate_pre * sigmoid_g
    hidden = (activated * up_pre).astype(jnp.bfloat16)
    part_out = jnp.dot(hidden, down_w, preferred_element_type=jnp.float32).astype(jnp.bfloat16)
    part_out, hidden, gate_pre, up_pre = lax.optimization_barrier((part_out, hidden, gate_pre, up_pre))
    sigmoid_g = jax.nn.sigmoid(gate_pre)
    activated = gate_pre * sigmoid_g
    out_rows = gather_back(part_out, groups).astype(jnp.float32)
    grad_hidden = contract_last(rows_c, down_w)
    grad_upin = (grad_hidden * activated).astype(jnp.bfloat16)
    grad_gatein = (grad_hidden * up_pre * sigmoid_g * (1.0 + gate_pre * (1.0 - sigmoid_g))).astype(
        jnp.bfloat16
    )
    part_dx = (contract_last(grad_gatein, gate_w) + contract_last(grad_upin, up_w)).astype(
        jnp.bfloat16
    )
    dx_rows = gather_back(part_dx, groups).astype(jnp.float32)
    new_gate = contract_first(rows_x, grad_gatein).astype(jnp.bfloat16)[None]
    new_up = contract_first(rows_x, grad_upin).astype(jnp.bfloat16)[None]
    new_down = contract_first(hidden, rows_c).astype(jnp.bfloat16)[None]
    owner = (token_of[None, :] == jnp.arange(tok_count, dtype=jnp.int32)[:, None]).astype(
        jnp.float32
    )
    layer_out = jnp.dot(
        owner * prob_rows[None, :],
        out_rows,
        precision=lax.Precision.HIGHEST,
        preferred_element_type=jnp.float32,
    ).astype(jnp.bfloat16)
    grad_tokens = jnp.dot(
        owner, dx_rows, precision=lax.Precision.HIGHEST, preferred_element_type=jnp.float32
    ).astype(jnp.bfloat16)
    score_rows = jnp.sum(rows_dy.astype(jnp.float32) * out_rows, axis=1)
    grad_probs = (
        jnp.zeros((flat_count + 1,), jnp.float32)
        .at[slots]
        .set(score_rows)[:flat_count]
        .reshape(tok_count, top_k)
    )
    return (layer_out, grad_tokens, grad_probs, new_gate, new_up, new_down)


def solution(mesh):
    return jax.shard_map(
        on_device,
        mesh=mesh,
        in_specs=(
            P(("dp", "expert"), None),
            P(("dp", "expert"), None),
            P(("dp", "expert"), None),
            P(("dp", "expert"), None),
            P("expert", None, "dp"),
            P("expert", None, "dp"),
            P("expert", "dp", None),
        ),
        out_specs=(
            P(("dp", "expert"), None),
            P(("dp", "expert"), None),
            P(("dp", "expert"), None),
            P("expert", None, "dp"),
            P("expert", None, "dp"),
            P("expert", "dp", None),
        ),
        check_vma=False,
    )
```

```python
import jax
import jax.numpy as jnp
from jax import lax
from jax.sharding import PartitionSpec as P


def slot_table(flat_ids, experts, capacity, sentinel):
    matches = (flat_ids[:, None] == jnp.arange(experts, dtype=jnp.int32)[None, :]).astype(jnp.int32)
    earlier = jnp.cumsum(matches, axis=0) - matches
    slot_pos = jnp.sum(earlier * matches, axis=1)
    target = jnp.where(flat_ids < experts, flat_ids * capacity + slot_pos, experts * capacity)
    flat_index = jnp.arange(flat_ids.shape[0], dtype=jnp.int32)
    blank_table = jnp.full((experts * capacity,), sentinel, jnp.int32)
    return blank_table.at[target].set(flat_index, mode="drop")


def contract_last(left, right):
    return lax.dot_general(
        left, right, (((1,), (1,)), ((), ())), preferred_element_type=jnp.float32
    )


def contract_first(left, right):
    return lax.dot_general(
        left, right, (((0,), (0,)), ((), ())), preferred_element_type=jnp.float32
    )


def along_expert(send_rows):
    return lax.all_to_all(send_rows, "expert", split_axis=0, concat_axis=0, tiled=True)


def replicate_dp(rows, groups):
    return lax.all_to_all(jnp.tile(rows, (groups, 1)), "dp", split_axis=0, concat_axis=0, tiled=True)


def gather_back(partial_rows, groups):
    by_group = lax.all_to_all(partial_rows, "dp", split_axis=0, concat_axis=0, tiled=True)
    rows = by_group.shape[0] // groups
    summed = jnp.sum(by_group.astype(jnp.float32).reshape(groups, rows, -1), axis=0)
    summed = summed.astype(jnp.bfloat16)
    return lax.all_to_all(summed, "expert", split_axis=0, concat_axis=0, tiled=True)


def on_device(tokens, gate_probs, expert_ids, cotangent, w_gate, w_up, w_down):
    tok_count, model_width = tokens.shape
    top_k = expert_ids.shape[1]
    experts = lax.axis_size("expert")
    groups = lax.axis_size("dp")
    capacity = 3 * tok_count * top_k // (16 * experts)
    flat_count = tok_count * top_k
    slots = slot_table(expert_ids.reshape(-1), experts, capacity, flat_count)
    token_of = slots // top_k
    zero_row = jnp.zeros((1, model_width), jnp.bfloat16)
    send_x = jnp.concatenate([tokens, zero_row], 0)[token_of]
    rows_dy = jnp.concatenate([cotangent, zero_row], 0)[token_of]
    prob_rows = jnp.concatenate([gate_probs.reshape(-1), jnp.zeros((1,), jnp.float32)], 0)[slots]
    send_c = (prob_rows[:, None] * rows_dy.astype(jnp.float32)).astype(jnp.bfloat16)
    rows_x = replicate_dp(along_expert(send_x), groups)
    rows_x, c_along = lax.optimization_barrier((rows_x, along_expert(send_c)))
    rows_c = replicate_dp(c_along, groups)
    gate_w = w_gate[0]
    up_w = w_up[0]
    down_w = w_down[0]
    gate_pre = jnp.dot(rows_x, gate_w, preferred_element_type=jnp.float32)
    up_pre = jnp.dot(rows_x, up_w, preferred_element_type=jnp.float32)
    sigmoid_g = jax.nn.sigmoid(gate_pre)
    activated = gate_pre * sigmoid_g
    hidden = (activated * up_pre).astype(jnp.bfloat16)
    part_out = jnp.dot(hidden, down_w, preferred_element_type=jnp.float32).astype(jnp.bfloat16)
    part_out, hidden, gate_pre, up_pre = lax.optimization_barrier((part_out, hidden, gate_pre, up_pre))
    sigmoid_g = jax.nn.sigmoid(gate_pre)
    activated = gate_pre * sigmoid_g
    out_rows = gather_back(part_out, groups).astype(jnp.float32)
    grad_hidden = contract_last(rows_c, down_w)
    grad_upin = (grad_hidden * activated).astype(jnp.bfloat16)
    grad_gatein = (grad_hidden * up_pre * sigmoid_g * (1.0 + gate_pre * (1.0 - sigmoid_g))).astype(
        jnp.bfloat16
    )
    part_dx = (contract_last(grad_gatein, gate_w) + contract_last(grad_upin, up_w)).astype(
        jnp.bfloat16
    )
    dx_rows = gather_back(part_dx, groups).astype(jnp.float32)
    new_gate = contract_first(rows_x, grad_gatein).astype(jnp.bfloat16)[None]
    new_up = contract_first(rows_x, grad_upin).astype(jnp.bfloat16)[None]
    new_down = contract_first(hidden, rows_c).astype(jnp.bfloat16)[None]
    owner = (token_of[None, :] == jnp.arange(tok_count, dtype=jnp.int32)[:, None]).astype(
        jnp.float32
    )
    layer_out = jnp.dot(
        owner * prob_rows[None, :],
        out_rows,
        precision=lax.Precision.HIGHEST,
        preferred_element_type=jnp.float32,
    ).astype(jnp.bfloat16)
    grad_tokens = jnp.dot(
        owner, dx_rows, precision=lax.Precision.HIGHEST, preferred_element_type=jnp.float32
    ).astype(jnp.bfloat16)
    score_rows = jnp.sum(rows_dy.astype(jnp.float32) * out_rows, axis=1)
    grad_probs = (
        jnp.zeros((flat_count + 1,), jnp.float32)
        .at[slots]
        .set(score_rows)[:flat_count]
        .reshape(tok_count, top_k)
    )
    return (layer_out, grad_tokens, grad_probs, new_gate, new_up, new_down)


def solution(mesh):
    return jax.shard_map(
        on_device,
        mesh=mesh,
        in_specs=(
            P(("dp", "expert"), None),
            P(("dp", "expert"), None),
            P(("dp", "expert"), None),
            P(("dp", "expert"), None),
            P("expert", None, "dp"),
            P("expert", None, "dp"),
            P("expert", "dp", None),
        ),
        out_specs=(
            P(("dp", "expert"), None),
            P(("dp", "expert"), None),
            P(("dp", "expert"), None),
            P("expert", None, "dp"),
            P("expert", None, "dp"),
            P("expert", "dp", None),
        ),
        check_vma=False,
    )
```

```python
import jax
import jax.numpy as jnp
from jax import lax
from jax.sharding import PartitionSpec as P


def slot_table(flat_ids, experts, capacity, sentinel):
    matches = (flat_ids[:, None] == jnp.arange(experts, dtype=jnp.int32)[None, :]).astype(jnp.int32)
    earlier = jnp.cumsum(matches, axis=0) - matches
    slot_pos = jnp.sum(earlier * matches, axis=1)
    target = jnp.where(flat_ids < experts, flat_ids * capacity + slot_pos, experts * capacity)
    flat_index = jnp.arange(flat_ids.shape[0], dtype=jnp.int32)
    blank_table = jnp.full((experts * capacity,), sentinel, jnp.int32)
    return blank_table.at[target].set(flat_index, mode="drop")


def contract_last(left, right):
    return lax.dot_general(
        left, right, (((1,), (1,)), ((), ())), preferred_element_type=jnp.float32
    )


def contract_first(left, right):
    return lax.dot_general(
        left, right, (((0,), (0,)), ((), ())), preferred_element_type=jnp.float32
    )


def along_expert(send_rows):
    return lax.all_to_all(send_rows, "expert", split_axis=0, concat_axis=0, tiled=True)


def pairs(groups, bit):
    return [(g, g ^ bit) for g in range(groups)]


def replicate_dp(rows, groups):
    if groups != 4:
        return lax.all_gather(rows, "dp", axis=0, tiled=True)
    half = rows.shape[0] // 2
    from_x = lax.ppermute(rows, "dp", perm=pairs(groups, 1))
    from_y = lax.ppermute(rows, "dp", perm=pairs(groups, 2))
    diag_lo = lax.ppermute(from_x[:half], "dp", perm=pairs(groups, 2))
    diag_hi = lax.ppermute(from_y[half:], "dp", perm=pairs(groups, 1))
    return jnp.concatenate([rows, from_x, from_y, diag_lo, diag_hi], axis=0)


def reduce_dp(partial_rows, groups):
    if groups != 4:
        return lax.psum_scatter(partial_rows, "dp", scatter_dimension=0, tiled=True)
    own, to_x, to_y, to_diag = jnp.split(partial_rows, 4, axis=0)
    half = own.shape[0] // 2
    via_x = lax.ppermute(to_diag[:half], "dp", perm=pairs(groups, 1))
    via_y = lax.ppermute(to_diag[half:], "dp", perm=pairs(groups, 2))
    to_y = jnp.concatenate(
        [(to_y[:half].astype(jnp.float32) + via_x.astype(jnp.float32)).astype(jnp.bfloat16), to_y[half:]], 0
    )
    to_x = jnp.concatenate(
        [to_x[:half], (to_x[half:].astype(jnp.float32) + via_y.astype(jnp.float32)).astype(jnp.bfloat16)], 0
    )
    from_x = lax.ppermute(to_x, "dp", perm=pairs(groups, 1))
    from_y = lax.ppermute(to_y, "dp", perm=pairs(groups, 2))
    total = own.astype(jnp.float32) + from_x.astype(jnp.float32) + from_y.astype(jnp.float32)
    return total.astype(jnp.bfloat16)


def gather_back(partial_rows, groups):
    summed = reduce_dp(partial_rows, groups)
    return lax.all_to_all(summed, "expert", split_axis=0, concat_axis=0, tiled=True)


def on_device(tokens, gate_probs, expert_ids, cotangent, w_gate, w_up, w_down):
    tok_count, model_width = tokens.shape
    top_k = expert_ids.shape[1]
    experts = lax.axis_size("expert")
    groups = lax.axis_size("dp")
    capacity = 3 * tok_count * top_k // (16 * experts)
    flat_count = tok_count * top_k
    slots = slot_table(expert_ids.reshape(-1), experts, capacity, flat_count)
    token_of = slots // top_k
    zero_row = jnp.zeros((1, model_width), jnp.bfloat16)
    send_x = jnp.concatenate([tokens, zero_row], 0)[token_of]
    rows_dy = jnp.concatenate([cotangent, zero_row], 0)[token_of]
    prob_rows = jnp.concatenate([gate_probs.reshape(-1), jnp.zeros((1,), jnp.float32)], 0)[slots]
    send_c = (prob_rows[:, None] * rows_dy.astype(jnp.float32)).astype(jnp.bfloat16)
    rows_x = replicate_dp(along_expert(send_x), groups)
    rows_x, c_along = lax.optimization_barrier((rows_x, along_expert(send_c)))
    rows_c = replicate_dp(c_along, groups)
    gate_w = w_gate[0]
    up_w = w_up[0]
    down_w = w_down[0]
    gate_pre = jnp.dot(rows_x, gate_w, preferred_element_type=jnp.float32)
    up_pre = jnp.dot(rows_x, up_w, preferred_element_type=jnp.float32)
    sigmoid_g = jax.nn.sigmoid(gate_pre)
    activated = gate_pre * sigmoid_g
    hidden = (activated * up_pre).astype(jnp.bfloat16)
    part_out = jnp.dot(hidden, down_w, preferred_element_type=jnp.float32).astype(jnp.bfloat16)
    part_out, hidden, gate_pre, up_pre = lax.optimization_barrier((part_out, hidden, gate_pre, up_pre))
    sigmoid_g = jax.nn.sigmoid(gate_pre)
    activated = gate_pre * sigmoid_g
    out_rows = gather_back(part_out, groups).astype(jnp.float32)
    grad_hidden = contract_last(rows_c, down_w)
    grad_upin = (grad_hidden * activated).astype(jnp.bfloat16)
    grad_gatein = (grad_hidden * up_pre * sigmoid_g * (1.0 + gate_pre * (1.0 - sigmoid_g))).astype(
        jnp.bfloat16
    )
    part_dx = (contract_last(grad_gatein, gate_w) + contract_last(grad_upin, up_w)).astype(
        jnp.bfloat16
    )
    dx_rows = gather_back(part_dx, groups).astype(jnp.float32)
    new_gate = contract_first(rows_x, grad_gatein).astype(jnp.bfloat16)[None]
    new_up = contract_first(rows_x, grad_upin).astype(jnp.bfloat16)[None]
    new_down = contract_first(hidden, rows_c).astype(jnp.bfloat16)[None]
    owner = (token_of[None, :] == jnp.arange(tok_count, dtype=jnp.int32)[:, None]).astype(
        jnp.float32
    )
    layer_out = jnp.dot(
        owner * prob_rows[None, :],
        out_rows,
        precision=lax.Precision.HIGHEST,
        preferred_element_type=jnp.float32,
    ).astype(jnp.bfloat16)
    grad_tokens = jnp.dot(
        owner, dx_rows, precision=lax.Precision.HIGHEST, preferred_element_type=jnp.float32
    ).astype(jnp.bfloat16)
    score_rows = jnp.sum(rows_dy.astype(jnp.float32) * out_rows, axis=1)
    grad_probs = (
        jnp.zeros((flat_count + 1,), jnp.float32)
        .at[slots]
        .set(score_rows)[:flat_count]
        .reshape(tok_count, top_k)
    )
    return (layer_out, grad_tokens, grad_probs, new_gate, new_up, new_down)


def solution(mesh):
    return jax.shard_map(
        on_device,
        mesh=mesh,
        in_specs=(
            P(("dp", "expert"), None),
            P(("dp", "expert"), None),
            P(("dp", "expert"), None),
            P(("dp", "expert"), None),
            P("expert", None, "dp"),
            P("expert", None, "dp"),
            P("expert", "dp", None),
        ),
        out_specs=(
            P(("dp", "expert"), None),
            P(("dp", "expert"), None),
            P(("dp", "expert"), None),
            P("expert", None, "dp"),
            P("expert", None, "dp"),
            P("expert", "dp", None),
        ),
        check_vma=False,
    )
```

```python
import jax
import jax.numpy as jnp
from jax import lax
from jax.sharding import PartitionSpec as P


def slot_table(flat_ids, experts, capacity, sentinel):
    matches = (flat_ids[:, None] == jnp.arange(experts, dtype=jnp.int32)[None, :]).astype(jnp.int32)
    earlier = jnp.cumsum(matches, axis=0) - matches
    slot_pos = jnp.sum(earlier * matches, axis=1)
    target = jnp.where(flat_ids < experts, flat_ids * capacity + slot_pos, experts * capacity)
    flat_index = jnp.arange(flat_ids.shape[0], dtype=jnp.int32)
    blank_table = jnp.full((experts * capacity,), sentinel, jnp.int32)
    return blank_table.at[target].set(flat_index, mode="drop")


def contract_last(left, right):
    return lax.dot_general(
        left, right, (((1,), (1,)), ((), ())), preferred_element_type=jnp.float32
    )


def contract_first(left, right):
    return lax.dot_general(
        left, right, (((0,), (0,)), ((), ())), preferred_element_type=jnp.float32
    )


def along_expert(send_rows):
    return lax.all_to_all(send_rows, "expert", split_axis=0, concat_axis=0, tiled=True)


def pairs(groups, bit):
    return [(g, g ^ bit) for g in range(groups)]


def swap_halves_first(rows, groups):
    if groups != 4:
        return ()
    return (
        lax.ppermute(rows, "dp", perm=pairs(groups, 1)),
        lax.ppermute(rows, "dp", perm=pairs(groups, 2)),
    )


def swap_halves_second(rows, first, groups):
    if groups != 4:
        return lax.all_gather(rows, "dp", axis=0, tiled=True)
    from_x, from_y = first
    half = rows.shape[0] // 2
    diag_lo = lax.ppermute(from_x[:half], "dp", perm=pairs(groups, 2))
    diag_hi = lax.ppermute(from_y[half:], "dp", perm=pairs(groups, 1))
    return jnp.concatenate([rows, from_x, from_y, diag_lo, diag_hi], axis=0)


def replicate_dp(rows, groups):
    return swap_halves_second(rows, swap_halves_first(rows, groups), groups)


def reduce_first(partial_rows, groups):
    if groups != 4:
        return ()
    to_diag = jnp.split(partial_rows, 4, axis=0)[3]
    half = to_diag.shape[0] // 2
    return (
        lax.ppermute(to_diag[:half], "dp", perm=pairs(groups, 1)),
        lax.ppermute(to_diag[half:], "dp", perm=pairs(groups, 2)),
    )


def reduce_second(partial_rows, first, groups):
    if groups != 4:
        return lax.psum_scatter(partial_rows, "dp", scatter_dimension=0, tiled=True)
    own, to_x, to_y, _ = jnp.split(partial_rows, 4, axis=0)
    via_x, via_y = first
    half = own.shape[0] // 2
    to_y = jnp.concatenate(
        [(to_y[:half].astype(jnp.float32) + via_x.astype(jnp.float32)).astype(jnp.bfloat16), to_y[half:]], 0
    )
    to_x = jnp.concatenate(
        [to_x[:half], (to_x[half:].astype(jnp.float32) + via_y.astype(jnp.float32)).astype(jnp.bfloat16)], 0
    )
    from_x = lax.ppermute(to_x, "dp", perm=pairs(groups, 1))
    from_y = lax.ppermute(to_y, "dp", perm=pairs(groups, 2))
    total = own.astype(jnp.float32) + from_x.astype(jnp.float32) + from_y.astype(jnp.float32)
    return total.astype(jnp.bfloat16)


def reduce_dp(partial_rows, groups):
    return reduce_second(partial_rows, reduce_first(partial_rows, groups), groups)


def gather_back(partial_rows, groups):
    summed = reduce_dp(partial_rows, groups)
    return lax.all_to_all(summed, "expert", split_axis=0, concat_axis=0, tiled=True)


def on_device(tokens, gate_probs, expert_ids, cotangent, w_gate, w_up, w_down):
    tok_count, model_width = tokens.shape
    top_k = expert_ids.shape[1]
    experts = lax.axis_size("expert")
    groups = lax.axis_size("dp")
    capacity = 3 * tok_count * top_k // (16 * experts)
    flat_count = tok_count * top_k
    slots = slot_table(expert_ids.reshape(-1), experts, capacity, flat_count)
    token_of = slots // top_k
    zero_row = jnp.zeros((1, model_width), jnp.bfloat16)
    send_x = jnp.concatenate([tokens, zero_row], 0)[token_of]
    rows_dy = jnp.concatenate([cotangent, zero_row], 0)[token_of]
    prob_rows = jnp.concatenate([gate_probs.reshape(-1), jnp.zeros((1,), jnp.float32)], 0)[slots]
    send_c = (prob_rows[:, None] * rows_dy.astype(jnp.float32)).astype(jnp.bfloat16)
    rows_x = replicate_dp(along_expert(send_x), groups)
    rows_x, c_along = lax.optimization_barrier((rows_x, along_expert(send_c)))
    c_first = swap_halves_first(c_along, groups)
    gate_w = w_gate[0]
    up_w = w_up[0]
    down_w = w_down[0]
    gate_pre = jnp.dot(rows_x, gate_w, preferred_element_type=jnp.float32)
    up_pre = jnp.dot(rows_x, up_w, preferred_element_type=jnp.float32)
    sigmoid_g = jax.nn.sigmoid(gate_pre)
    activated = gate_pre * sigmoid_g
    hidden = (activated * up_pre).astype(jnp.bfloat16)
    part_out = jnp.dot(hidden, down_w, preferred_element_type=jnp.float32).astype(jnp.bfloat16)
    part_out, hidden, gate_pre, up_pre, c_first = lax.optimization_barrier(
        (part_out, hidden, gate_pre, up_pre, c_first)
    )
    sigmoid_g = jax.nn.sigmoid(gate_pre)
    activated = gate_pre * sigmoid_g
    out_first = reduce_first(part_out, groups)
    rows_c = swap_halves_second(c_along, c_first, groups)
    rows_c, out_first = lax.optimization_barrier((rows_c, out_first))
    out_home = reduce_second(part_out, out_first, groups)
    grad_hidden = contract_last(rows_c, down_w)
    grad_upin = (grad_hidden * activated).astype(jnp.bfloat16)
    grad_gatein = (grad_hidden * up_pre * sigmoid_g * (1.0 + gate_pre * (1.0 - sigmoid_g))).astype(
        jnp.bfloat16
    )
    part_dx = (contract_last(grad_gatein, gate_w) + contract_last(grad_upin, up_w)).astype(
        jnp.bfloat16
    )
    part_dx, grad_upin, grad_gatein, out_home = lax.optimization_barrier(
        (part_dx, grad_upin, grad_gatein, out_home)
    )
    out_rows = along_expert(out_home).astype(jnp.float32)
    dx_rows = gather_back(part_dx, groups).astype(jnp.float32)
    new_gate = contract_first(rows_x, grad_gatein).astype(jnp.bfloat16)[None]
    new_up = contract_first(rows_x, grad_upin).astype(jnp.bfloat16)[None]
    new_down = contract_first(hidden, rows_c).astype(jnp.bfloat16)[None]
    owner = (token_of[None, :] == jnp.arange(tok_count, dtype=jnp.int32)[:, None]).astype(
        jnp.float32
    )
    layer_out = jnp.dot(
        owner * prob_rows[None, :],
        out_rows,
        precision=lax.Precision.HIGHEST,
        preferred_element_type=jnp.float32,
    ).astype(jnp.bfloat16)
    grad_tokens = jnp.dot(
        owner, dx_rows, precision=lax.Precision.HIGHEST, preferred_element_type=jnp.float32
    ).astype(jnp.bfloat16)
    score_rows = jnp.sum(rows_dy.astype(jnp.float32) * out_rows, axis=1)
    grad_probs = (
        jnp.zeros((flat_count + 1,), jnp.float32)
        .at[slots]
        .set(score_rows)[:flat_count]
        .reshape(tok_count, top_k)
    )
    return (layer_out, grad_tokens, grad_probs, new_gate, new_up, new_down)


def solution(mesh):
    return jax.shard_map(
        on_device,
        mesh=mesh,
        in_specs=(
            P(("dp", "expert"), None),
            P(("dp", "expert"), None),
            P(("dp", "expert"), None),
            P(("dp", "expert"), None),
            P("expert", None, "dp"),
            P("expert", None, "dp"),
            P("expert", "dp", None),
        ),
        out_specs=(
            P(("dp", "expert"), None),
            P(("dp", "expert"), None),
            P(("dp", "expert"), None),
            P("expert", None, "dp"),
            P("expert", None, "dp"),
            P("expert", "dp", None),
        ),
        check_vma=False,
    )
```

```python
import jax
import jax.numpy as jnp
from jax import lax
from jax.sharding import PartitionSpec as P


def slot_selection(flat_ids, experts, capacity):
    matches = (flat_ids[:, None] == jnp.arange(experts, dtype=jnp.int32)[None, :]).astype(jnp.int32)
    earlier = jnp.cumsum(matches, axis=0) - matches
    slot_pos = jnp.sum(earlier * matches, axis=1)
    target = jnp.where(flat_ids < experts, flat_ids * capacity + slot_pos, -1)
    return target[:, None] == jnp.arange(experts * capacity, dtype=jnp.int32)[None, :]


def contract_last(left, right):
    return lax.dot_general(
        left, right, (((1,), (1,)), ((), ())), preferred_element_type=jnp.float32
    )


def contract_first(left, right):
    return lax.dot_general(
        left, right, (((0,), (0,)), ((), ())), preferred_element_type=jnp.float32
    )


def along_expert(send_rows):
    return lax.all_to_all(send_rows, "expert", split_axis=0, concat_axis=0, tiled=True)


def pairs(groups, bit):
    return [(g, g ^ bit) for g in range(groups)]


def swap_halves_first(rows, groups):
    if groups != 4:
        return ()
    return (
        lax.ppermute(rows, "dp", perm=pairs(groups, 1)),
        lax.ppermute(rows, "dp", perm=pairs(groups, 2)),
    )


def swap_halves_second(rows, first, groups):
    if groups != 4:
        return lax.all_gather(rows, "dp", axis=0, tiled=True)
    from_x, from_y = first
    half = rows.shape[0] // 2
    diag_lo = lax.ppermute(from_x[:half], "dp", perm=pairs(groups, 2))
    diag_hi = lax.ppermute(from_y[half:], "dp", perm=pairs(groups, 1))
    return jnp.concatenate([rows, from_x, from_y, diag_lo, diag_hi], axis=0)


def replicate_dp(rows, groups):
    return swap_halves_second(rows, swap_halves_first(rows, groups), groups)


def reduce_first(partial_rows, groups):
    if groups != 4:
        return ()
    to_diag = jnp.split(partial_rows, 4, axis=0)[3]
    half = to_diag.shape[0] // 2
    return (
        lax.ppermute(to_diag[:half], "dp", perm=pairs(groups, 1)),
        lax.ppermute(to_diag[half:], "dp", perm=pairs(groups, 2)),
    )


def reduce_second(partial_rows, first, groups):
    if groups != 4:
        return lax.psum_scatter(partial_rows, "dp", scatter_dimension=0, tiled=True)
    own, to_x, to_y, _ = jnp.split(partial_rows, 4, axis=0)
    via_x, via_y = first
    half = own.shape[0] // 2
    to_y = jnp.concatenate(
        [(to_y[:half].astype(jnp.float32) + via_x.astype(jnp.float32)).astype(jnp.bfloat16), to_y[half:]], 0
    )
    to_x = jnp.concatenate(
        [to_x[:half], (to_x[half:].astype(jnp.float32) + via_y.astype(jnp.float32)).astype(jnp.bfloat16)], 0
    )
    from_x = lax.ppermute(to_x, "dp", perm=pairs(groups, 1))
    from_y = lax.ppermute(to_y, "dp", perm=pairs(groups, 2))
    total = own.astype(jnp.float32) + from_x.astype(jnp.float32) + from_y.astype(jnp.float32)
    return total.astype(jnp.bfloat16)


def reduce_dp(partial_rows, groups):
    return reduce_second(partial_rows, reduce_first(partial_rows, groups), groups)


def gather_back(partial_rows, groups):
    summed = reduce_dp(partial_rows, groups)
    return lax.all_to_all(summed, "expert", split_axis=0, concat_axis=0, tiled=True)


def on_device(tokens, gate_probs, expert_ids, cotangent, w_gate, w_up, w_down):
    tok_count, model_width = tokens.shape
    top_k = expert_ids.shape[1]
    experts = lax.axis_size("expert")
    groups = lax.axis_size("dp")
    capacity = 3 * tok_count * top_k // (16 * experts)
    chosen = slot_selection(expert_ids.reshape(-1), experts, capacity)
    owner = jnp.any(chosen.reshape(tok_count, top_k, -1), axis=1).astype(jnp.bfloat16)
    send_x = contract_first(owner, tokens).astype(jnp.bfloat16)
    rows_dy = contract_first(owner, cotangent).astype(jnp.bfloat16)
    prob_rows = jnp.sum(jnp.where(chosen, gate_probs.reshape(-1)[:, None], 0.0), axis=0)
    send_c = (prob_rows[:, None] * rows_dy.astype(jnp.float32)).astype(jnp.bfloat16)
    rows_x = replicate_dp(along_expert(send_x), groups)
    rows_x, c_along = lax.optimization_barrier((rows_x, along_expert(send_c)))
    c_first = swap_halves_first(c_along, groups)
    gate_w = w_gate[0]
    up_w = w_up[0]
    down_w = w_down[0]
    gate_pre = jnp.dot(rows_x, gate_w, preferred_element_type=jnp.float32)
    up_pre = jnp.dot(rows_x, up_w, preferred_element_type=jnp.float32)
    sigmoid_g = jax.nn.sigmoid(gate_pre)
    activated = gate_pre * sigmoid_g
    hidden = (activated * up_pre).astype(jnp.bfloat16)
    part_out = jnp.dot(hidden, down_w, preferred_element_type=jnp.float32).astype(jnp.bfloat16)
    part_out, hidden, gate_pre, up_pre, c_first = lax.optimization_barrier(
        (part_out, hidden, gate_pre, up_pre, c_first)
    )
    sigmoid_g = jax.nn.sigmoid(gate_pre)
    activated = gate_pre * sigmoid_g
    out_first = reduce_first(part_out, groups)
    rows_c = swap_halves_second(c_along, c_first, groups)
    rows_c, out_first = lax.optimization_barrier((rows_c, out_first))
    out_home = reduce_second(part_out, out_first, groups)
    grad_hidden = contract_last(rows_c, down_w)
    grad_upin = (grad_hidden * activated).astype(jnp.bfloat16)
    grad_gatein = (grad_hidden * up_pre * sigmoid_g * (1.0 + gate_pre * (1.0 - sigmoid_g))).astype(
        jnp.bfloat16
    )
    part_dx = (contract_last(grad_gatein, gate_w) + contract_last(grad_upin, up_w)).astype(
        jnp.bfloat16
    )
    part_dx, grad_upin, grad_gatein, out_home = lax.optimization_barrier(
        (part_dx, grad_upin, grad_gatein, out_home)
    )
    out_rows = along_expert(out_home).astype(jnp.float32)
    dx_rows = gather_back(part_dx, groups)
    new_gate = contract_first(rows_x, grad_gatein).astype(jnp.bfloat16)[None]
    new_up = contract_first(rows_x, grad_upin).astype(jnp.bfloat16)[None]
    new_down = contract_first(hidden, rows_c).astype(jnp.bfloat16)[None]
    layer_out = jnp.dot(
        owner.astype(jnp.float32) * prob_rows[None, :],
        out_rows,
        precision=lax.Precision.HIGHEST,
        preferred_element_type=jnp.float32,
    ).astype(jnp.bfloat16)
    grad_tokens = jnp.dot(owner, dx_rows, preferred_element_type=jnp.float32).astype(jnp.bfloat16)
    score_rows = jnp.sum(rows_dy.astype(jnp.float32) * out_rows, axis=1)
    grad_probs = jnp.sum(jnp.where(chosen, score_rows[None, :], 0.0), axis=1).reshape(tok_count, top_k)
    return (layer_out, grad_tokens, grad_probs, new_gate, new_up, new_down)


def solution(mesh):
    return jax.shard_map(
        on_device,
        mesh=mesh,
        in_specs=(
            P(("dp", "expert"), None),
            P(("dp", "expert"), None),
            P(("dp", "expert"), None),
            P(("dp", "expert"), None),
            P("expert", None, "dp"),
            P("expert", None, "dp"),
            P("expert", "dp", None),
        ),
        out_specs=(
            P(("dp", "expert"), None),
            P(("dp", "expert"), None),
            P(("dp", "expert"), None),
            P("expert", None, "dp"),
            P("expert", None, "dp"),
            P("expert", "dp", None),
        ),
        check_vma=False,
    )
```

```python
import jax
import jax.numpy as jnp
from jax import lax
from jax.sharding import PartitionSpec as P


def slot_selection(flat_ids, experts, capacity):
    matches = (flat_ids[:, None] == jnp.arange(experts, dtype=jnp.int32)[None, :]).astype(jnp.int32)
    earlier = jnp.cumsum(matches, axis=0) - matches
    slot_pos = jnp.sum(earlier * matches, axis=1)
    target = jnp.where(flat_ids < experts, flat_ids * capacity + slot_pos, -1)
    return target[:, None] == jnp.arange(experts * capacity, dtype=jnp.int32)[None, :]


def contract_last(left, right):
    return lax.dot_general(
        left, right, (((1,), (1,)), ((), ())), preferred_element_type=jnp.float32
    )


def contract_first(left, right):
    return lax.dot_general(
        left, right, (((0,), (0,)), ((), ())), preferred_element_type=jnp.float32
    )


def along_expert(send_rows, by_shifts=False):
    experts = lax.axis_size("expert")
    if experts != 8 or not by_shifts:
        return lax.all_to_all(send_rows, "expert", split_axis=0, concat_axis=0, tiled=True)
    blocks = send_rows.reshape(experts, -1, send_rows.shape[-1])
    me = lax.axis_index("expert")
    shifts = jnp.arange(experts, dtype=jnp.int32)
    outgoing = jnp.take(blocks, (me + shifts) % experts, axis=0)
    received = [outgoing[0]]
    for shift in range(1, experts):
        perm = [(i, (i + shift) % experts) for i in range(experts)]
        received.append(lax.ppermute(outgoing[shift], "expert", perm=perm))
    by_shift = jnp.stack(received, axis=0)
    by_source = jnp.take(by_shift, (me - shifts) % experts, axis=0)
    return by_source.reshape(send_rows.shape)


def pairs(groups, bit):
    return [(g, g ^ bit) for g in range(groups)]


def swap_halves_first(rows, groups):
    if groups != 4:
        return ()
    return (
        lax.ppermute(rows, "dp", perm=pairs(groups, 1)),
        lax.ppermute(rows, "dp", perm=pairs(groups, 2)),
    )


def swap_halves_second(rows, first, groups):
    if groups != 4:
        return lax.all_gather(rows, "dp", axis=0, tiled=True)
    from_x, from_y = first
    half = rows.shape[0] // 2
    diag_lo = lax.ppermute(from_x[:half], "dp", perm=pairs(groups, 2))
    diag_hi = lax.ppermute(from_y[half:], "dp", perm=pairs(groups, 1))
    return jnp.concatenate([rows, from_x, from_y, diag_lo, diag_hi], axis=0)


def replicate_dp(rows, groups):
    return swap_halves_second(rows, swap_halves_first(rows, groups), groups)


def reduce_first(partial_rows, groups):
    if groups != 4:
        return ()
    to_diag = jnp.split(partial_rows, 4, axis=0)[3]
    half = to_diag.shape[0] // 2
    return (
        lax.ppermute(to_diag[:half], "dp", perm=pairs(groups, 1)),
        lax.ppermute(to_diag[half:], "dp", perm=pairs(groups, 2)),
    )


def reduce_second(partial_rows, first, groups):
    if groups != 4:
        return lax.psum_scatter(partial_rows, "dp", scatter_dimension=0, tiled=True)
    own, to_x, to_y, _ = jnp.split(partial_rows, 4, axis=0)
    via_x, via_y = first
    half = own.shape[0] // 2
    to_y = jnp.concatenate(
        [(to_y[:half].astype(jnp.float32) + via_x.astype(jnp.float32)).astype(jnp.bfloat16), to_y[half:]], 0
    )
    to_x = jnp.concatenate(
        [to_x[:half], (to_x[half:].astype(jnp.float32) + via_y.astype(jnp.float32)).astype(jnp.bfloat16)], 0
    )
    from_x = lax.ppermute(to_x, "dp", perm=pairs(groups, 1))
    from_y = lax.ppermute(to_y, "dp", perm=pairs(groups, 2))
    total = own.astype(jnp.float32) + from_x.astype(jnp.float32) + from_y.astype(jnp.float32)
    return total.astype(jnp.bfloat16)


def reduce_dp(partial_rows, groups):
    return reduce_second(partial_rows, reduce_first(partial_rows, groups), groups)


def gather_back(partial_rows, groups):
    summed = reduce_dp(partial_rows, groups)
    return lax.all_to_all(summed, "expert", split_axis=0, concat_axis=0, tiled=True)


def on_device(tokens, gate_probs, expert_ids, cotangent, w_gate, w_up, w_down):
    tok_count, model_width = tokens.shape
    top_k = expert_ids.shape[1]
    experts = lax.axis_size("expert")
    groups = lax.axis_size("dp")
    capacity = 3 * tok_count * top_k // (16 * experts)
    chosen = slot_selection(expert_ids.reshape(-1), experts, capacity)
    owner = jnp.any(chosen.reshape(tok_count, top_k, -1), axis=1).astype(jnp.bfloat16)
    send_x = contract_first(owner, tokens).astype(jnp.bfloat16)
    rows_dy = contract_first(owner, cotangent).astype(jnp.bfloat16)
    prob_rows = jnp.sum(jnp.where(chosen, gate_probs.reshape(-1)[:, None], 0.0), axis=0)
    send_c = (prob_rows[:, None] * rows_dy.astype(jnp.float32)).astype(jnp.bfloat16)
    rows_x = replicate_dp(along_expert(send_x, by_shifts=True), groups)
    rows_x, c_along = lax.optimization_barrier((rows_x, along_expert(send_c)))
    c_first = swap_halves_first(c_along, groups)
    gate_w = w_gate[0]
    up_w = w_up[0]
    down_w = w_down[0]
    gate_pre = jnp.dot(rows_x, gate_w, preferred_element_type=jnp.float32)
    up_pre = jnp.dot(rows_x, up_w, preferred_element_type=jnp.float32)
    sigmoid_g = jax.nn.sigmoid(gate_pre)
    activated = gate_pre * sigmoid_g
    hidden = (activated * up_pre).astype(jnp.bfloat16)
    part_out = jnp.dot(hidden, down_w, preferred_element_type=jnp.float32).astype(jnp.bfloat16)
    part_out, hidden, gate_pre, up_pre, c_first = lax.optimization_barrier(
        (part_out, hidden, gate_pre, up_pre, c_first)
    )
    sigmoid_g = jax.nn.sigmoid(gate_pre)
    activated = gate_pre * sigmoid_g
    out_first = reduce_first(part_out, groups)
    rows_c = swap_halves_second(c_along, c_first, groups)
    rows_c, out_first = lax.optimization_barrier((rows_c, out_first))
    out_home = reduce_second(part_out, out_first, groups)
    grad_hidden = contract_last(rows_c, down_w)
    grad_upin = (grad_hidden * activated).astype(jnp.bfloat16)
    grad_gatein = (grad_hidden * up_pre * sigmoid_g * (1.0 + gate_pre * (1.0 - sigmoid_g))).astype(
        jnp.bfloat16
    )
    part_dx = (contract_last(grad_gatein, gate_w) + contract_last(grad_upin, up_w)).astype(
        jnp.bfloat16
    )
    part_dx, grad_upin, grad_gatein, out_home = lax.optimization_barrier(
        (part_dx, grad_upin, grad_gatein, out_home)
    )
    out_rows = along_expert(out_home).astype(jnp.float32)
    dx_rows = gather_back(part_dx, groups)
    new_gate = contract_first(rows_x, grad_gatein).astype(jnp.bfloat16)[None]
    new_up = contract_first(rows_x, grad_upin).astype(jnp.bfloat16)[None]
    new_down = contract_first(hidden, rows_c).astype(jnp.bfloat16)[None]
    layer_out = jnp.dot(
        owner.astype(jnp.float32) * prob_rows[None, :],
        out_rows,
        precision=lax.Precision.HIGHEST,
        preferred_element_type=jnp.float32,
    ).astype(jnp.bfloat16)
    grad_tokens = jnp.dot(owner, dx_rows, preferred_element_type=jnp.float32).astype(jnp.bfloat16)
    score_rows = jnp.sum(rows_dy.astype(jnp.float32) * out_rows, axis=1)
    grad_probs = jnp.sum(jnp.where(chosen, score_rows[None, :], 0.0), axis=1).reshape(tok_count, top_k)
    return (layer_out, grad_tokens, grad_probs, new_gate, new_up, new_down)


def solution(mesh):
    return jax.shard_map(
        on_device,
        mesh=mesh,
        in_specs=(
            P(("dp", "expert"), None),
            P(("dp", "expert"), None),
            P(("dp", "expert"), None),
            P(("dp", "expert"), None),
            P("expert", None, "dp"),
            P("expert", None, "dp"),
            P("expert", "dp", None),
        ),
        out_specs=(
            P(("dp", "expert"), None),
            P(("dp", "expert"), None),
            P(("dp", "expert"), None),
            P("expert", None, "dp"),
            P("expert", None, "dp"),
            P("expert", "dp", None),
        ),
        check_vma=False,
    )
```

```python
import jax
import jax.numpy as jnp
from jax import lax
from jax.sharding import PartitionSpec as P


def slot_selection(flat_ids, experts, capacity):
    matches = (flat_ids[:, None] == jnp.arange(experts, dtype=jnp.int32)[None, :]).astype(jnp.int32)
    earlier = jnp.cumsum(matches, axis=0) - matches
    slot_pos = jnp.sum(earlier * matches, axis=1)
    target = jnp.where(flat_ids < experts, flat_ids * capacity + slot_pos, -1)
    return target[:, None] == jnp.arange(experts * capacity, dtype=jnp.int32)[None, :]


def contract_last(left, right):
    return lax.dot_general(
        left, right, (((1,), (1,)), ((), ())), preferred_element_type=jnp.float32
    )


def contract_first(left, right):
    return lax.dot_general(
        left, right, (((0,), (0,)), ((), ())), preferred_element_type=jnp.float32
    )


def along_expert(send_rows):
    return lax.all_to_all(send_rows, "expert", split_axis=0, concat_axis=0, tiled=True)


def pairs(groups, bit):
    return [(g, g ^ bit) for g in range(groups)]


def swap_halves_first(rows, groups):
    if groups != 4:
        return ()
    return (
        lax.ppermute(rows, "dp", perm=pairs(groups, 1)),
        lax.ppermute(rows, "dp", perm=pairs(groups, 2)),
    )


def swap_halves_second(rows, first, groups):
    if groups != 4:
        return lax.all_gather(rows, "dp", axis=0, tiled=True)
    from_x, from_y = first
    half = rows.shape[0] // 2
    diag_lo = lax.ppermute(from_x[:half], "dp", perm=pairs(groups, 2))
    diag_hi = lax.ppermute(from_y[half:], "dp", perm=pairs(groups, 1))
    return jnp.concatenate([rows, from_x, from_y, diag_lo, diag_hi], axis=0)


def replicate_dp(rows, groups):
    return swap_halves_second(rows, swap_halves_first(rows, groups), groups)


def reduce_first(partial_rows, groups):
    if groups != 4:
        return ()
    to_diag = jnp.split(partial_rows, 4, axis=0)[3]
    half = to_diag.shape[0] // 2
    return (
        lax.ppermute(to_diag[:half], "dp", perm=pairs(groups, 1)),
        lax.ppermute(to_diag[half:], "dp", perm=pairs(groups, 2)),
    )


def reduce_second(partial_rows, first, groups):
    if groups != 4:
        return lax.psum_scatter(partial_rows, "dp", scatter_dimension=0, tiled=True)
    own, to_x, to_y, _ = jnp.split(partial_rows, 4, axis=0)
    via_x, via_y = first
    half = own.shape[0] // 2
    to_y = jnp.concatenate(
        [(to_y[:half].astype(jnp.float32) + via_x.astype(jnp.float32)).astype(jnp.bfloat16), to_y[half:]], 0
    )
    to_x = jnp.concatenate(
        [to_x[:half], (to_x[half:].astype(jnp.float32) + via_y.astype(jnp.float32)).astype(jnp.bfloat16)], 0
    )
    from_x = lax.ppermute(to_x, "dp", perm=pairs(groups, 1))
    from_y = lax.ppermute(to_y, "dp", perm=pairs(groups, 2))
    total = own.astype(jnp.float32) + from_x.astype(jnp.float32) + from_y.astype(jnp.float32)
    return total.astype(jnp.bfloat16)


def reduce_dp(partial_rows, groups):
    return reduce_second(partial_rows, reduce_first(partial_rows, groups), groups)


def gather_back(partial_rows, groups):
    summed = reduce_dp(partial_rows, groups)
    return lax.all_to_all(summed, "expert", split_axis=0, concat_axis=0, tiled=True)


def on_device(tokens, gate_probs, expert_ids, cotangent, w_gate, w_up, w_down):
    tok_count, model_width = tokens.shape
    top_k = expert_ids.shape[1]
    experts = lax.axis_size("expert")
    groups = lax.axis_size("dp")
    capacity = 3 * tok_count * top_k // (16 * experts)
    chosen = slot_selection(expert_ids.reshape(-1), experts, capacity)
    owner = jnp.any(chosen.reshape(tok_count, top_k, -1), axis=1).astype(jnp.bfloat16)
    send_x = contract_first(owner, tokens).astype(jnp.bfloat16)
    rows_dy = contract_first(owner, cotangent).astype(jnp.bfloat16)
    prob_rows = jnp.sum(jnp.where(chosen, gate_probs.reshape(-1)[:, None], 0.0), axis=0)
    send_c = (prob_rows[:, None] * rows_dy.astype(jnp.float32)).astype(jnp.bfloat16)
    send_x, send_c = lax.optimization_barrier((send_x, send_c))
    rows_x = replicate_dp(along_expert(send_x), groups)
    rows_x, c_along = lax.optimization_barrier((rows_x, along_expert(send_c)))
    c_first = swap_halves_first(c_along, groups)
    gate_w = w_gate[0]
    up_w = w_up[0]
    down_w = w_down[0]
    gate_pre = jnp.dot(rows_x, gate_w, preferred_element_type=jnp.float32)
    up_pre = jnp.dot(rows_x, up_w, preferred_element_type=jnp.float32)
    sigmoid_g = jax.nn.sigmoid(gate_pre)
    activated = gate_pre * sigmoid_g
    hidden = (activated * up_pre).astype(jnp.bfloat16)
    part_out = jnp.dot(hidden, down_w, preferred_element_type=jnp.float32).astype(jnp.bfloat16)
    part_out, hidden, gate_pre, up_pre, c_first = lax.optimization_barrier(
        (part_out, hidden, gate_pre, up_pre, c_first)
    )
    sigmoid_g = jax.nn.sigmoid(gate_pre)
    activated = gate_pre * sigmoid_g
    out_first = reduce_first(part_out, groups)
    rows_c = swap_halves_second(c_along, c_first, groups)
    rows_c, out_first = lax.optimization_barrier((rows_c, out_first))
    out_home = reduce_second(part_out, out_first, groups)
    grad_hidden = contract_last(rows_c, down_w)
    grad_upin = (grad_hidden * activated).astype(jnp.bfloat16)
    grad_gatein = (grad_hidden * up_pre * sigmoid_g * (1.0 + gate_pre * (1.0 - sigmoid_g))).astype(
        jnp.bfloat16
    )
    part_dx = (contract_last(grad_gatein, gate_w) + contract_last(grad_upin, up_w)).astype(
        jnp.bfloat16
    )
    part_dx, grad_upin, grad_gatein, out_home = lax.optimization_barrier(
        (part_dx, grad_upin, grad_gatein, out_home)
    )
    out_rows = along_expert(out_home).astype(jnp.float32)
    dx_rows = gather_back(part_dx, groups)
    new_gate = contract_first(rows_x, grad_gatein).astype(jnp.bfloat16)[None]
    new_up = contract_first(rows_x, grad_upin).astype(jnp.bfloat16)[None]
    new_down = contract_first(hidden, rows_c).astype(jnp.bfloat16)[None]
    layer_out = jnp.dot(
        owner.astype(jnp.float32) * prob_rows[None, :],
        out_rows,
        precision=lax.Precision.HIGHEST,
        preferred_element_type=jnp.float32,
    ).astype(jnp.bfloat16)
    grad_tokens = jnp.dot(owner, dx_rows, preferred_element_type=jnp.float32).astype(jnp.bfloat16)
    score_rows = jnp.sum(rows_dy.astype(jnp.float32) * out_rows, axis=1)
    grad_probs = jnp.sum(jnp.where(chosen, score_rows[None, :], 0.0), axis=1).reshape(tok_count, top_k)
    return (layer_out, grad_tokens, grad_probs, new_gate, new_up, new_down)


def solution(mesh):
    return jax.shard_map(
        on_device,
        mesh=mesh,
        in_specs=(
            P(("dp", "expert"), None),
            P(("dp", "expert"), None),
            P(("dp", "expert"), None),
            P(("dp", "expert"), None),
            P("expert", None, "dp"),
            P("expert", None, "dp"),
            P("expert", "dp", None),
        ),
        out_specs=(
            P(("dp", "expert"), None),
            P(("dp", "expert"), None),
            P(("dp", "expert"), None),
            P("expert", None, "dp"),
            P("expert", None, "dp"),
            P("expert", "dp", None),
        ),
        check_vma=False,
    )
```

```python
import jax
import jax.numpy as jnp
from jax import lax
from jax.sharding import PartitionSpec as P


def slot_selection(flat_ids, experts, capacity):
    matches = (flat_ids[:, None] == jnp.arange(experts, dtype=jnp.int32)[None, :]).astype(jnp.int32)
    earlier = jnp.cumsum(matches, axis=0) - matches
    slot_pos = jnp.sum(earlier * matches, axis=1)
    target = jnp.where(flat_ids < experts, flat_ids * capacity + slot_pos, -1)
    return target[:, None] == jnp.arange(experts * capacity, dtype=jnp.int32)[None, :]


def contract_last(left, right):
    return lax.dot_general(
        left, right, (((1,), (1,)), ((), ())), preferred_element_type=jnp.float32
    )


def contract_first(left, right):
    return lax.dot_general(
        left, right, (((0,), (0,)), ((), ())), preferred_element_type=jnp.float32
    )


def along_expert(send_rows):
    return lax.all_to_all(send_rows, "expert", split_axis=0, concat_axis=0, tiled=True)


def pairs(groups, bit):
    return [(g, g ^ bit) for g in range(groups)]


def swap_halves_first(rows, groups):
    if groups != 4:
        return ()
    return (
        lax.ppermute(rows, "dp", perm=pairs(groups, 1)),
        lax.ppermute(rows, "dp", perm=pairs(groups, 2)),
    )


def swap_halves_second(rows, first, groups):
    if groups != 4:
        return lax.all_gather(rows, "dp", axis=0, tiled=True)
    from_x, from_y = first
    half = rows.shape[0] // 2
    diag_lo = lax.ppermute(from_x[:half], "dp", perm=pairs(groups, 2))
    diag_hi = lax.ppermute(from_y[half:], "dp", perm=pairs(groups, 1))
    return jnp.concatenate([rows, from_x, from_y, diag_lo, diag_hi], axis=0)


def replicate_dp(rows, groups):
    return swap_halves_second(rows, swap_halves_first(rows, groups), groups)


def reduce_first(partial_rows, groups):
    if groups != 4:
        return ()
    to_diag = jnp.split(partial_rows, 4, axis=0)[3]
    half = to_diag.shape[0] // 2
    return (
        lax.ppermute(to_diag[:half], "dp", perm=pairs(groups, 1)),
        lax.ppermute(to_diag[half:], "dp", perm=pairs(groups, 2)),
    )


def reduce_second(partial_rows, first, groups):
    if groups != 4:
        return lax.psum_scatter(partial_rows, "dp", scatter_dimension=0, tiled=True)
    own, to_x, to_y, _ = jnp.split(partial_rows, 4, axis=0)
    via_x, via_y = first
    half = own.shape[0] // 2
    to_y = jnp.concatenate(
        [(to_y[:half].astype(jnp.float32) + via_x.astype(jnp.float32)).astype(jnp.bfloat16), to_y[half:]], 0
    )
    to_x = jnp.concatenate(
        [to_x[:half], (to_x[half:].astype(jnp.float32) + via_y.astype(jnp.float32)).astype(jnp.bfloat16)], 0
    )
    from_x = lax.ppermute(to_x, "dp", perm=pairs(groups, 1))
    from_y = lax.ppermute(to_y, "dp", perm=pairs(groups, 2))
    total = own.astype(jnp.float32) + from_x.astype(jnp.float32) + from_y.astype(jnp.float32)
    return total.astype(jnp.bfloat16)


def reduce_dp(partial_rows, groups):
    return reduce_second(partial_rows, reduce_first(partial_rows, groups), groups)


def gather_back(partial_rows, groups):
    summed = reduce_dp(partial_rows, groups)
    return lax.all_to_all(summed, "expert", split_axis=0, concat_axis=0, tiled=True)


def on_device(tokens, gate_probs, expert_ids, cotangent, w_gate, w_up, w_down):
    tok_count, model_width = tokens.shape
    top_k = expert_ids.shape[1]
    experts = lax.axis_size("expert")
    groups = lax.axis_size("dp")
    capacity = 3 * tok_count * top_k // (16 * experts)
    chosen = slot_selection(expert_ids.reshape(-1), experts, capacity)
    owner = jnp.any(chosen.reshape(tok_count, top_k, -1), axis=1).astype(jnp.bfloat16)
    send_x = contract_first(owner, tokens).astype(jnp.bfloat16)
    rows_dy = contract_first(owner, cotangent).astype(jnp.bfloat16)
    prob_rows = jnp.sum(jnp.where(chosen, gate_probs.reshape(-1)[:, None], 0.0), axis=0)
    send_c = (prob_rows[:, None] * rows_dy.astype(jnp.float32)).astype(jnp.bfloat16)
    rows_x = replicate_dp(along_expert(send_x), groups)
    rows_x, c_along = lax.optimization_barrier((rows_x, along_expert(send_c)))
    c_first = swap_halves_first(c_along, groups)
    gate_w = w_gate[0]
    up_w = w_up[0]
    down_w = w_down[0]
    gate_pre = jnp.dot(rows_x, gate_w, preferred_element_type=jnp.float32)
    up_pre = jnp.dot(rows_x, up_w, preferred_element_type=jnp.float32)
    sigmoid_g = jax.nn.sigmoid(gate_pre)
    activated = gate_pre * sigmoid_g
    hidden = (activated * up_pre).astype(jnp.bfloat16)
    part_out = jnp.dot(hidden, down_w, preferred_element_type=jnp.float32).astype(jnp.bfloat16)
    part_out, hidden, gate_pre, up_pre, c_first = lax.optimization_barrier(
        (part_out, hidden, gate_pre, up_pre, c_first)
    )
    sigmoid_g = jax.nn.sigmoid(gate_pre)
    activated = gate_pre * sigmoid_g
    out_first = reduce_first(part_out, groups)
    rows_c = swap_halves_second(c_along, c_first, groups)
    rows_c, out_first = lax.optimization_barrier((rows_c, out_first))
    out_home = reduce_second(part_out, out_first, groups)
    grad_hidden = contract_last(rows_c, down_w)
    grad_upin = (grad_hidden * activated).astype(jnp.bfloat16)
    grad_gatein = (grad_hidden * up_pre * sigmoid_g * (1.0 + gate_pre * (1.0 - sigmoid_g))).astype(
        jnp.bfloat16
    )
    part_dx = (contract_last(grad_gatein, gate_w) + contract_last(grad_upin, up_w)).astype(
        jnp.bfloat16
    )
    part_dx, grad_upin, grad_gatein, out_home = lax.optimization_barrier(
        (part_dx, grad_upin, grad_gatein, out_home)
    )
    out_rows = along_expert(out_home).astype(jnp.float32)
    new_gate = contract_first(rows_x, grad_gatein).astype(jnp.bfloat16)[None]
    new_up = contract_first(rows_x, grad_upin).astype(jnp.bfloat16)[None]
    new_down = contract_first(hidden, rows_c).astype(jnp.bfloat16)[None]
    dx_home, new_gate, new_up, new_down = lax.optimization_barrier(
        (reduce_dp(part_dx, groups), new_gate, new_up, new_down)
    )
    dx_rows = along_expert(dx_home)
    layer_out = jnp.dot(
        owner.astype(jnp.float32) * prob_rows[None, :],
        out_rows,
        precision=lax.Precision.HIGHEST,
        preferred_element_type=jnp.float32,
    ).astype(jnp.bfloat16)
    grad_tokens = jnp.dot(owner, dx_rows, preferred_element_type=jnp.float32).astype(jnp.bfloat16)
    score_rows = jnp.sum(rows_dy.astype(jnp.float32) * out_rows, axis=1)
    grad_probs = jnp.sum(jnp.where(chosen, score_rows[None, :], 0.0), axis=1).reshape(tok_count, top_k)
    return (layer_out, grad_tokens, grad_probs, new_gate, new_up, new_down)


def solution(mesh):
    return jax.shard_map(
        on_device,
        mesh=mesh,
        in_specs=(
            P(("dp", "expert"), None),
            P(("dp", "expert"), None),
            P(("dp", "expert"), None),
            P(("dp", "expert"), None),
            P("expert", None, "dp"),
            P("expert", None, "dp"),
            P("expert", "dp", None),
        ),
        out_specs=(
            P(("dp", "expert"), None),
            P(("dp", "expert"), None),
            P(("dp", "expert"), None),
            P("expert", None, "dp"),
            P("expert", None, "dp"),
            P("expert", "dp", None),
        ),
        check_vma=False,
    )
```

```python
import jax
import jax.numpy as jnp
from jax import lax
from jax.sharding import PartitionSpec as P


def slot_selection(flat_ids, experts, capacity):
    matches = (flat_ids[:, None] == jnp.arange(experts, dtype=jnp.int32)[None, :]).astype(jnp.int32)
    earlier = jnp.cumsum(matches, axis=0) - matches
    slot_pos = jnp.sum(earlier * matches, axis=1)
    target = jnp.where(flat_ids < experts, flat_ids * capacity + slot_pos, -1)
    return target[:, None] == jnp.arange(experts * capacity, dtype=jnp.int32)[None, :]


def contract_last(left, right):
    return lax.dot_general(
        left, right, (((1,), (1,)), ((), ())), preferred_element_type=jnp.float32
    )


def contract_first(left, right):
    return lax.dot_general(
        left, right, (((0,), (0,)), ((), ())), preferred_element_type=jnp.float32
    )


def along_expert(send_rows):
    return lax.all_to_all(send_rows, "expert", split_axis=0, concat_axis=0, tiled=True)


def pairs(groups, bit):
    return [(g, g ^ bit) for g in range(groups)]


def swap_halves_first(rows, groups):
    if groups != 4:
        return ()
    return (
        lax.ppermute(rows, "dp", perm=pairs(groups, 1)),
        lax.ppermute(rows, "dp", perm=pairs(groups, 2)),
    )


def swap_halves_second(rows, first, groups):
    if groups != 4:
        return lax.all_gather(rows, "dp", axis=0, tiled=True)
    from_x, from_y = first
    half = rows.shape[0] // 2
    diag_lo = lax.ppermute(from_x[:half], "dp", perm=pairs(groups, 2))
    diag_hi = lax.ppermute(from_y[half:], "dp", perm=pairs(groups, 1))
    return jnp.concatenate([rows, from_x, from_y, diag_lo, diag_hi], axis=0)


def replicate_dp(rows, groups):
    return swap_halves_second(rows, swap_halves_first(rows, groups), groups)


def reduce_first(partial_rows, groups):
    if groups != 4:
        return ()
    to_diag = jnp.split(partial_rows, 4, axis=0)[3]
    half = to_diag.shape[0] // 2
    return (
        lax.ppermute(to_diag[:half], "dp", perm=pairs(groups, 1)),
        lax.ppermute(to_diag[half:], "dp", perm=pairs(groups, 2)),
    )


def reduce_second(partial_rows, first, groups):
    if groups != 4:
        return lax.psum_scatter(partial_rows, "dp", scatter_dimension=0, tiled=True)
    own, to_x, to_y, _ = jnp.split(partial_rows, 4, axis=0)
    via_x, via_y = first
    half = own.shape[0] // 2
    to_y = jnp.concatenate(
        [(to_y[:half].astype(jnp.float32) + via_x.astype(jnp.float32)).astype(jnp.bfloat16), to_y[half:]], 0
    )
    to_x = jnp.concatenate(
        [to_x[:half], (to_x[half:].astype(jnp.float32) + via_y.astype(jnp.float32)).astype(jnp.bfloat16)], 0
    )
    from_x = lax.ppermute(to_x, "dp", perm=pairs(groups, 1))
    from_y = lax.ppermute(to_y, "dp", perm=pairs(groups, 2))
    return own, from_x, from_y


def add_parts(parts):
    if not isinstance(parts, tuple):
        return parts
    own, from_x, from_y = parts
    total = own.astype(jnp.float32) + from_x.astype(jnp.float32) + from_y.astype(jnp.float32)
    return total.astype(jnp.bfloat16)


def reduce_dp(partial_rows, groups):
    return add_parts(reduce_second(partial_rows, reduce_first(partial_rows, groups), groups))


def gather_back(partial_rows, groups):
    summed = reduce_dp(partial_rows, groups)
    return lax.all_to_all(summed, "expert", split_axis=0, concat_axis=0, tiled=True)


def on_device(tokens, gate_probs, expert_ids, cotangent, w_gate, w_up, w_down):
    tok_count, model_width = tokens.shape
    top_k = expert_ids.shape[1]
    experts = lax.axis_size("expert")
    groups = lax.axis_size("dp")
    capacity = 3 * tok_count * top_k // (16 * experts)
    chosen = slot_selection(expert_ids.reshape(-1), experts, capacity)
    owner = jnp.any(chosen.reshape(tok_count, top_k, -1), axis=1).astype(jnp.bfloat16)
    send_x = contract_first(owner, tokens).astype(jnp.bfloat16)
    rows_dy = contract_first(owner, cotangent).astype(jnp.bfloat16)
    prob_rows = jnp.sum(jnp.where(chosen, gate_probs.reshape(-1)[:, None], 0.0), axis=0)
    send_c = (prob_rows[:, None] * rows_dy.astype(jnp.float32)).astype(jnp.bfloat16)
    rows_x = replicate_dp(along_expert(send_x), groups)
    rows_x, c_along = lax.optimization_barrier((rows_x, along_expert(send_c)))
    c_first = swap_halves_first(c_along, groups)
    gate_w = w_gate[0]
    up_w = w_up[0]
    down_w = w_down[0]
    gate_pre = jnp.dot(rows_x, gate_w, preferred_element_type=jnp.float32)
    up_pre = jnp.dot(rows_x, up_w, preferred_element_type=jnp.float32)
    sigmoid_g = jax.nn.sigmoid(gate_pre)
    activated = gate_pre * sigmoid_g
    hidden = (activated * up_pre).astype(jnp.bfloat16)
    part_out = jnp.dot(hidden, down_w, preferred_element_type=jnp.float32).astype(jnp.bfloat16)
    part_out, hidden, gate_pre, up_pre, c_first = lax.optimization_barrier(
        (part_out, hidden, gate_pre, up_pre, c_first)
    )
    sigmoid_g = jax.nn.sigmoid(gate_pre)
    activated = gate_pre * sigmoid_g
    out_first = reduce_first(part_out, groups)
    rows_c = swap_halves_second(c_along, c_first, groups)
    rows_c, out_first = lax.optimization_barrier((rows_c, out_first))
    out_parts = reduce_second(part_out, out_first, groups)
    grad_hidden = contract_last(rows_c, down_w)
    grad_upin = (grad_hidden * activated).astype(jnp.bfloat16)
    grad_gatein = (grad_hidden * up_pre * sigmoid_g * (1.0 + gate_pre * (1.0 - sigmoid_g))).astype(
        jnp.bfloat16
    )
    part_dx = (contract_last(grad_gatein, gate_w) + contract_last(grad_upin, up_w)).astype(
        jnp.bfloat16
    )
    part_dx, grad_upin, grad_gatein, out_parts = lax.optimization_barrier(
        (part_dx, grad_upin, grad_gatein, out_parts)
    )
    out_rows = along_expert(add_parts(out_parts)).astype(jnp.float32)
    new_gate = contract_first(rows_x, grad_gatein).astype(jnp.bfloat16)[None]
    new_up = contract_first(rows_x, grad_upin).astype(jnp.bfloat16)[None]
    new_down = contract_first(hidden, rows_c).astype(jnp.bfloat16)[None]
    dx_home, new_gate, new_up, new_down = lax.optimization_barrier(
        (reduce_dp(part_dx, groups), new_gate, new_up, new_down)
    )
    dx_rows = along_expert(dx_home)
    layer_out = jnp.dot(
        owner.astype(jnp.float32) * prob_rows[None, :],
        out_rows,
        precision=lax.Precision.HIGHEST,
        preferred_element_type=jnp.float32,
    ).astype(jnp.bfloat16)
    grad_tokens = jnp.dot(owner, dx_rows, preferred_element_type=jnp.float32).astype(jnp.bfloat16)
    score_rows = jnp.sum(rows_dy.astype(jnp.float32) * out_rows, axis=1)
    grad_probs = jnp.sum(jnp.where(chosen, score_rows[None, :], 0.0), axis=1).reshape(tok_count, top_k)
    return (layer_out, grad_tokens, grad_probs, new_gate, new_up, new_down)


def solution(mesh):
    return jax.shard_map(
        on_device,
        mesh=mesh,
        in_specs=(
            P(("dp", "expert"), None),
            P(("dp", "expert"), None),
            P(("dp", "expert"), None),
            P(("dp", "expert"), None),
            P("expert", None, "dp"),
            P("expert", None, "dp"),
            P("expert", "dp", None),
        ),
        out_specs=(
            P(("dp", "expert"), None),
            P(("dp", "expert"), None),
            P(("dp", "expert"), None),
            P("expert", None, "dp"),
            P("expert", None, "dp"),
            P("expert", "dp", None),
        ),
        check_vma=False,
    )
```

```python
import jax
import jax.numpy as jnp
from jax import lax
from jax.sharding import PartitionSpec as P


def slot_selection(flat_ids, experts, capacity):
    matches = (flat_ids[:, None] == jnp.arange(experts, dtype=jnp.int32)[None, :]).astype(jnp.int32)
    earlier = jnp.cumsum(matches, axis=0) - matches
    slot_pos = jnp.sum(earlier * matches, axis=1)
    target = jnp.where(flat_ids < experts, flat_ids * capacity + slot_pos, -1)
    return target[:, None] == jnp.arange(experts * capacity, dtype=jnp.int32)[None, :]


def contract_last(left, right):
    return lax.dot_general(
        left, right, (((1,), (1,)), ((), ())), preferred_element_type=jnp.float32
    )


def contract_first(left, right):
    return lax.dot_general(
        left, right, (((0,), (0,)), ((), ())), preferred_element_type=jnp.float32
    )


def along_expert(send_rows):
    return lax.all_to_all(send_rows, "expert", split_axis=0, concat_axis=0, tiled=True)


def pairs(groups, bit):
    return [(g, g ^ bit) for g in range(groups)]


def swap_halves_first(rows, groups):
    if groups != 4:
        return ()
    return (
        lax.ppermute(rows, "dp", perm=pairs(groups, 1)),
        lax.ppermute(rows, "dp", perm=pairs(groups, 2)),
    )


def swap_halves_second(rows, first, groups):
    if groups != 4:
        return lax.all_gather(rows, "dp", axis=0, tiled=True)
    from_x, from_y = first
    half = rows.shape[0] // 2
    diag_lo = lax.ppermute(from_x[:half], "dp", perm=pairs(groups, 2))
    diag_hi = lax.ppermute(from_y[half:], "dp", perm=pairs(groups, 1))
    return jnp.concatenate([rows, from_x, from_y, diag_lo, diag_hi], axis=0)


def replicate_dp(rows, groups):
    return swap_halves_second(rows, swap_halves_first(rows, groups), groups)


def reduce_first(partial_rows, groups):
    if groups != 4:
        return ()
    to_diag = jnp.split(partial_rows, 4, axis=0)[3]
    half = to_diag.shape[0] // 2
    return (
        lax.ppermute(to_diag[:half], "dp", perm=pairs(groups, 1)),
        lax.ppermute(to_diag[half:], "dp", perm=pairs(groups, 2)),
    )


def reduce_second(partial_rows, first, groups):
    if groups != 4:
        return lax.psum_scatter(partial_rows, "dp", scatter_dimension=0, tiled=True)
    own, to_x, to_y, _ = jnp.split(partial_rows, 4, axis=0)
    via_x, via_y = first
    half = own.shape[0] // 2
    to_y = jnp.concatenate(
        [(to_y[:half].astype(jnp.float32) + via_x.astype(jnp.float32)).astype(jnp.bfloat16), to_y[half:]], 0
    )
    to_x = jnp.concatenate(
        [to_x[:half], (to_x[half:].astype(jnp.float32) + via_y.astype(jnp.float32)).astype(jnp.bfloat16)], 0
    )
    from_x = lax.ppermute(to_x, "dp", perm=pairs(groups, 1))
    from_y = lax.ppermute(to_y, "dp", perm=pairs(groups, 2))
    return own, from_x, from_y


def add_parts(parts):
    if not isinstance(parts, tuple):
        return parts
    own, from_x, from_y = parts
    total = own.astype(jnp.float32) + from_x.astype(jnp.float32) + from_y.astype(jnp.float32)
    return total.astype(jnp.bfloat16)


def reduce_dp(partial_rows, groups):
    return add_parts(reduce_second(partial_rows, reduce_first(partial_rows, groups), groups))


def gather_back(partial_rows, groups):
    summed = reduce_dp(partial_rows, groups)
    return lax.all_to_all(summed, "expert", split_axis=0, concat_axis=0, tiled=True)


def on_device(tokens, gate_probs, expert_ids, cotangent, w_gate, w_up, w_down):
    tok_count, model_width = tokens.shape
    top_k = expert_ids.shape[1]
    experts = lax.axis_size("expert")
    groups = lax.axis_size("dp")
    capacity = 3 * tok_count * top_k // (16 * experts)
    chosen = slot_selection(expert_ids.reshape(-1), experts, capacity)
    owner = jnp.any(chosen.reshape(tok_count, top_k, -1), axis=1).astype(jnp.bfloat16)
    send_x = contract_first(owner, tokens).astype(jnp.bfloat16)
    rows_dy = contract_first(owner, cotangent).astype(jnp.bfloat16)
    prob_rows = jnp.sum(jnp.where(chosen, gate_probs.reshape(-1)[:, None], 0.0), axis=0)
    send_c = (prob_rows[:, None] * rows_dy.astype(jnp.float32)).astype(jnp.bfloat16)
    rows_x = replicate_dp(along_expert(send_x), groups)
    rows_x, c_along = lax.optimization_barrier((rows_x, along_expert(send_c)))
    c_first = swap_halves_first(c_along, groups)
    gate_w = w_gate[0]
    up_w = w_up[0]
    down_w = w_down[0]
    gate_pre = jnp.dot(rows_x, gate_w, preferred_element_type=jnp.float32)
    up_pre = jnp.dot(rows_x, up_w, preferred_element_type=jnp.float32)
    sigmoid_g = jax.nn.sigmoid(gate_pre)
    activated = gate_pre * sigmoid_g
    hidden = (activated * up_pre).astype(jnp.bfloat16)
    part_out = jnp.dot(hidden, down_w, preferred_element_type=jnp.float32).astype(jnp.bfloat16)
    part_out, hidden, gate_pre, up_pre, c_first = lax.optimization_barrier(
        (part_out, hidden, gate_pre, up_pre, c_first)
    )
    sigmoid_g = jax.nn.sigmoid(gate_pre)
    activated = gate_pre * sigmoid_g
    out_first = reduce_first(part_out, groups)
    rows_c = swap_halves_second(c_along, c_first, groups)
    rows_c, out_first = lax.optimization_barrier((rows_c, out_first))
    out_parts = reduce_second(part_out, out_first, groups)
    grad_hidden = contract_last(rows_c, down_w)
    grad_upin = (grad_hidden * activated).astype(jnp.bfloat16)
    grad_gatein = (grad_hidden * up_pre * sigmoid_g * (1.0 + gate_pre * (1.0 - sigmoid_g))).astype(
        jnp.bfloat16
    )
    part_dx = (contract_last(grad_gatein, gate_w) + contract_last(grad_upin, up_w)).astype(
        jnp.bfloat16
    )
    dx_first = reduce_first(part_dx, groups)
    dx_first, out_parts = lax.optimization_barrier((dx_first, out_parts))
    out_rows = along_expert(add_parts(out_parts)).astype(jnp.float32)
    new_gate = contract_first(rows_x, grad_gatein).astype(jnp.bfloat16)[None]
    new_up = contract_first(rows_x, grad_upin).astype(jnp.bfloat16)[None]
    new_down = contract_first(hidden, rows_c).astype(jnp.bfloat16)[None]
    dx_home, new_gate, new_up, new_down = lax.optimization_barrier(
        (add_parts(reduce_second(part_dx, dx_first, groups)), new_gate, new_up, new_down)
    )
    dx_rows = along_expert(dx_home)
    layer_out = jnp.dot(
        owner.astype(jnp.float32) * prob_rows[None, :],
        out_rows,
        precision=lax.Precision.HIGHEST,
        preferred_element_type=jnp.float32,
    ).astype(jnp.bfloat16)
    grad_tokens = jnp.dot(owner, dx_rows, preferred_element_type=jnp.float32).astype(jnp.bfloat16)
    score_rows = jnp.sum(rows_dy.astype(jnp.float32) * out_rows, axis=1)
    grad_probs = jnp.sum(jnp.where(chosen, score_rows[None, :], 0.0), axis=1).reshape(tok_count, top_k)
    return (layer_out, grad_tokens, grad_probs, new_gate, new_up, new_down)


def solution(mesh):
    return jax.shard_map(
        on_device,
        mesh=mesh,
        in_specs=(
            P(("dp", "expert"), None),
            P(("dp", "expert"), None),
            P(("dp", "expert"), None),
            P(("dp", "expert"), None),
            P("expert", None, "dp"),
            P("expert", None, "dp"),
            P("expert", "dp", None),
        ),
        out_specs=(
            P(("dp", "expert"), None),
            P(("dp", "expert"), None),
            P(("dp", "expert"), None),
            P("expert", None, "dp"),
            P("expert", None, "dp"),
            P("expert", "dp", None),
        ),
        check_vma=False,
    )
```

```python
import jax
import jax.numpy as jnp
from jax import lax
from jax.sharding import PartitionSpec as P


def slot_selection(flat_ids, experts, capacity):
    matches = (flat_ids[:, None] == jnp.arange(experts, dtype=jnp.int32)[None, :]).astype(jnp.int32)
    earlier = jnp.cumsum(matches, axis=0) - matches
    slot_pos = jnp.sum(earlier * matches, axis=1)
    target = jnp.where(flat_ids < experts, flat_ids * capacity + slot_pos, -1)
    return target[:, None] == jnp.arange(experts * capacity, dtype=jnp.int32)[None, :]


def contract_last(left, right):
    return lax.dot_general(
        left, right, (((1,), (1,)), ((), ())), preferred_element_type=jnp.float32
    )


def contract_first(left, right):
    return lax.dot_general(
        left, right, (((0,), (0,)), ((), ())), preferred_element_type=jnp.float32
    )


def along_expert(send_rows):
    return lax.all_to_all(send_rows, "expert", split_axis=0, concat_axis=0, tiled=True)


def pairs(groups, bit):
    return [(g, g ^ bit) for g in range(groups)]


def swap_halves_first(rows, groups):
    if groups != 4:
        return ()
    half = rows.shape[0] // 2
    return tuple(
        lax.ppermute(part, "dp", perm=pairs(groups, bit))
        for bit in (1, 2)
        for part in (rows[:half], rows[half:])
    )


def swap_halves_second(rows, first, groups):
    if groups != 4:
        return lax.all_gather(rows, "dp", axis=0, tiled=True)
    x_lo, x_hi, y_lo, y_hi = first
    diag_lo = lax.ppermute(x_lo, "dp", perm=pairs(groups, 2))
    diag_hi = lax.ppermute(y_hi, "dp", perm=pairs(groups, 1))
    return jnp.concatenate([rows, x_lo, x_hi, y_lo, y_hi, diag_lo, diag_hi], axis=0)


def replicate_dp(rows, groups):
    return swap_halves_second(rows, swap_halves_first(rows, groups), groups)


def reduce_first(partial_rows, groups):
    if groups != 4:
        return ()
    to_diag = jnp.split(partial_rows, 4, axis=0)[3]
    half = to_diag.shape[0] // 2
    return (
        lax.ppermute(to_diag[:half], "dp", perm=pairs(groups, 1)),
        lax.ppermute(to_diag[half:], "dp", perm=pairs(groups, 2)),
    )


def reduce_second(partial_rows, first, groups):
    if groups != 4:
        return lax.psum_scatter(partial_rows, "dp", scatter_dimension=0, tiled=True)
    own, to_x, to_y, _ = jnp.split(partial_rows, 4, axis=0)
    via_x, via_y = first
    half = own.shape[0] // 2
    to_y = jnp.concatenate(
        [(to_y[:half].astype(jnp.float32) + via_x.astype(jnp.float32)).astype(jnp.bfloat16), to_y[half:]], 0
    )
    to_x = jnp.concatenate(
        [to_x[:half], (to_x[half:].astype(jnp.float32) + via_y.astype(jnp.float32)).astype(jnp.bfloat16)], 0
    )
    from_x = lax.ppermute(to_x, "dp", perm=pairs(groups, 1))
    from_y = lax.ppermute(to_y, "dp", perm=pairs(groups, 2))
    return own, from_x, from_y


def add_parts(parts):
    if not isinstance(parts, tuple):
        return parts
    own, from_x, from_y = parts
    total = own.astype(jnp.float32) + from_x.astype(jnp.float32) + from_y.astype(jnp.float32)
    return total.astype(jnp.bfloat16)


def reduce_dp(partial_rows, groups):
    return add_parts(reduce_second(partial_rows, reduce_first(partial_rows, groups), groups))


def gather_back(partial_rows, groups):
    summed = reduce_dp(partial_rows, groups)
    return lax.all_to_all(summed, "expert", split_axis=0, concat_axis=0, tiled=True)


def on_device(tokens, gate_probs, expert_ids, cotangent, w_gate, w_up, w_down):
    tok_count, model_width = tokens.shape
    top_k = expert_ids.shape[1]
    experts = lax.axis_size("expert")
    groups = lax.axis_size("dp")
    capacity = 3 * tok_count * top_k // (16 * experts)
    chosen = slot_selection(expert_ids.reshape(-1), experts, capacity)
    owner = jnp.any(chosen.reshape(tok_count, top_k, -1), axis=1).astype(jnp.bfloat16)
    send_x = contract_first(owner, tokens).astype(jnp.bfloat16)
    rows_dy = contract_first(owner, cotangent).astype(jnp.bfloat16)
    prob_rows = jnp.sum(jnp.where(chosen, gate_probs.reshape(-1)[:, None], 0.0), axis=0)
    send_c = (prob_rows[:, None] * rows_dy.astype(jnp.float32)).astype(jnp.bfloat16)
    rows_x = replicate_dp(along_expert(send_x), groups)
    rows_x, c_along = lax.optimization_barrier((rows_x, along_expert(send_c)))
    c_first = swap_halves_first(c_along, groups)
    gate_w = w_gate[0]
    up_w = w_up[0]
    down_w = w_down[0]
    gate_pre = jnp.dot(rows_x, gate_w, preferred_element_type=jnp.float32)
    up_pre = jnp.dot(rows_x, up_w, preferred_element_type=jnp.float32)
    sigmoid_g = jax.nn.sigmoid(gate_pre)
    activated = gate_pre * sigmoid_g
    hidden = (activated * up_pre).astype(jnp.bfloat16)
    part_out = jnp.dot(hidden, down_w, preferred_element_type=jnp.float32).astype(jnp.bfloat16)
    part_out, hidden, gate_pre, up_pre, c_first = lax.optimization_barrier(
        (part_out, hidden, gate_pre, up_pre, c_first)
    )
    sigmoid_g = jax.nn.sigmoid(gate_pre)
    activated = gate_pre * sigmoid_g
    out_first = reduce_first(part_out, groups)
    rows_c = swap_halves_second(c_along, c_first, groups)
    rows_c, out_first = lax.optimization_barrier((rows_c, out_first))
    out_parts = reduce_second(part_out, out_first, groups)
    grad_hidden = contract_last(rows_c, down_w)
    grad_upin = (grad_hidden * activated).astype(jnp.bfloat16)
    grad_gatein = (grad_hidden * up_pre * sigmoid_g * (1.0 + gate_pre * (1.0 - sigmoid_g))).astype(
        jnp.bfloat16
    )
    part_dx = (contract_last(grad_gatein, gate_w) + contract_last(grad_upin, up_w)).astype(
        jnp.bfloat16
    )
    part_dx, grad_upin, grad_gatein, out_parts = lax.optimization_barrier(
        (part_dx, grad_upin, grad_gatein, out_parts)
    )
    out_rows = along_expert(add_parts(out_parts)).astype(jnp.float32)
    new_gate = contract_first(rows_x, grad_gatein).astype(jnp.bfloat16)[None]
    new_up = contract_first(rows_x, grad_upin).astype(jnp.bfloat16)[None]
    new_down = contract_first(hidden, rows_c).astype(jnp.bfloat16)[None]
    dx_home, new_gate, new_up, new_down = lax.optimization_barrier(
        (reduce_dp(part_dx, groups), new_gate, new_up, new_down)
    )
    dx_rows = along_expert(dx_home)
    layer_out = jnp.dot(
        owner.astype(jnp.float32) * prob_rows[None, :],
        out_rows,
        precision=lax.Precision.HIGHEST,
        preferred_element_type=jnp.float32,
    ).astype(jnp.bfloat16)
    grad_tokens = jnp.dot(owner, dx_rows, preferred_element_type=jnp.float32).astype(jnp.bfloat16)
    score_rows = jnp.sum(rows_dy.astype(jnp.float32) * out_rows, axis=1)
    grad_probs = jnp.sum(jnp.where(chosen, score_rows[None, :], 0.0), axis=1).reshape(tok_count, top_k)
    return (layer_out, grad_tokens, grad_probs, new_gate, new_up, new_down)


def solution(mesh):
    return jax.shard_map(
        on_device,
        mesh=mesh,
        in_specs=(
            P(("dp", "expert"), None),
            P(("dp", "expert"), None),
            P(("dp", "expert"), None),
            P(("dp", "expert"), None),
            P("expert", None, "dp"),
            P("expert", None, "dp"),
            P("expert", "dp", None),
        ),
        out_specs=(
            P(("dp", "expert"), None),
            P(("dp", "expert"), None),
            P(("dp", "expert"), None),
            P("expert", None, "dp"),
            P("expert", None, "dp"),
            P("expert", "dp", None),
        ),
        check_vma=False,
    )
```

```python
import jax
import jax.numpy as jnp
from jax import lax
from jax.sharding import PartitionSpec as P


def slot_selection(flat_ids, experts, capacity):
    matches = (flat_ids[:, None] == jnp.arange(experts, dtype=jnp.int32)[None, :]).astype(jnp.int32)
    earlier = jnp.cumsum(matches, axis=0) - matches
    slot_pos = jnp.sum(earlier * matches, axis=1)
    target = jnp.where(flat_ids < experts, flat_ids * capacity + slot_pos, -1)
    return target[:, None] == jnp.arange(experts * capacity, dtype=jnp.int32)[None, :]


def contract_last(left, right):
    return lax.dot_general(
        left, right, (((1,), (1,)), ((), ())), preferred_element_type=jnp.float32
    )


def contract_first(left, right):
    return lax.dot_general(
        left, right, (((0,), (0,)), ((), ())), preferred_element_type=jnp.float32
    )


def along_expert(send_rows):
    return lax.all_to_all(send_rows, "expert", split_axis=0, concat_axis=0, tiled=True)


def pairs(groups, bit):
    return [(g, g ^ bit) for g in range(groups)]


def swap_halves_first(rows, groups):
    if groups != 4:
        return ()
    half = rows.shape[0] // 2
    return tuple(
        lax.ppermute(part, "dp", perm=pairs(groups, bit))
        for bit in (1, 2)
        for part in (rows[:half], rows[half:])
    )


def swap_halves_second(rows, first, groups):
    if groups != 4:
        return lax.all_gather(rows, "dp", axis=0, tiled=True)
    x_lo, x_hi, y_lo, y_hi = first
    diag_lo = lax.ppermute(x_lo, "dp", perm=pairs(groups, 2))
    diag_hi = lax.ppermute(y_hi, "dp", perm=pairs(groups, 1))
    return jnp.concatenate([rows, x_lo, x_hi, y_lo, y_hi, diag_lo, diag_hi], axis=0)


def replicate_dp(rows, groups):
    return swap_halves_second(rows, swap_halves_first(rows, groups), groups)


def reduce_first(partial_rows, groups):
    if groups != 4:
        return ()
    _, to_x, to_y, to_diag = jnp.split(partial_rows, 4, axis=0)
    half = to_diag.shape[0] // 2
    return (
        lax.ppermute(to_diag[:half], "dp", perm=pairs(groups, 1)),
        lax.ppermute(to_diag[half:], "dp", perm=pairs(groups, 2)),
        lax.ppermute(to_x[:half], "dp", perm=pairs(groups, 1)),
        lax.ppermute(to_y[half:], "dp", perm=pairs(groups, 2)),
    )


def reduce_second(partial_rows, first, groups):
    if groups != 4:
        return lax.psum_scatter(partial_rows, "dp", scatter_dimension=0, tiled=True)
    own, to_x, to_y, _ = jnp.split(partial_rows, 4, axis=0)
    via_x, via_y, from_x_lo, from_y_hi = first
    half = own.shape[0] // 2
    to_y_lo = (to_y[:half].astype(jnp.float32) + via_x.astype(jnp.float32)).astype(jnp.bfloat16)
    to_x_hi = (to_x[half:].astype(jnp.float32) + via_y.astype(jnp.float32)).astype(jnp.bfloat16)
    from_x_hi = lax.ppermute(to_x_hi, "dp", perm=pairs(groups, 1))
    from_y_lo = lax.ppermute(to_y_lo, "dp", perm=pairs(groups, 2))
    return own, from_x_lo, from_x_hi, from_y_lo, from_y_hi


def add_parts(parts):
    if not isinstance(parts, tuple):
        return parts
    own, from_x_lo, from_x_hi, from_y_lo, from_y_hi = [part.astype(jnp.float32) for part in parts]
    half = from_x_lo.shape[0]
    low = own[:half] + from_x_lo + from_y_lo
    high = own[half:] + from_x_hi + from_y_hi
    return jnp.concatenate([low, high], axis=0).astype(jnp.bfloat16)


def reduce_dp(partial_rows, groups):
    return add_parts(reduce_second(partial_rows, reduce_first(partial_rows, groups), groups))


def gather_back(partial_rows, groups):
    summed = reduce_dp(partial_rows, groups)
    return lax.all_to_all(summed, "expert", split_axis=0, concat_axis=0, tiled=True)


def on_device(tokens, gate_probs, expert_ids, cotangent, w_gate, w_up, w_down):
    tok_count, model_width = tokens.shape
    top_k = expert_ids.shape[1]
    experts = lax.axis_size("expert")
    groups = lax.axis_size("dp")
    capacity = 3 * tok_count * top_k // (16 * experts)
    chosen = slot_selection(expert_ids.reshape(-1), experts, capacity)
    owner = jnp.any(chosen.reshape(tok_count, top_k, -1), axis=1).astype(jnp.bfloat16)
    send_x = contract_first(owner, tokens).astype(jnp.bfloat16)
    rows_dy = contract_first(owner, cotangent).astype(jnp.bfloat16)
    prob_rows = jnp.sum(jnp.where(chosen, gate_probs.reshape(-1)[:, None], 0.0), axis=0)
    send_c = (prob_rows[:, None] * rows_dy.astype(jnp.float32)).astype(jnp.bfloat16)
    rows_x = replicate_dp(along_expert(send_x), groups)
    rows_x, c_along = lax.optimization_barrier((rows_x, along_expert(send_c)))
    c_first = swap_halves_first(c_along, groups)
    gate_w = w_gate[0]
    up_w = w_up[0]
    down_w = w_down[0]
    gate_pre = jnp.dot(rows_x, gate_w, preferred_element_type=jnp.float32)
    up_pre = jnp.dot(rows_x, up_w, preferred_element_type=jnp.float32)
    sigmoid_g = jax.nn.sigmoid(gate_pre)
    activated = gate_pre * sigmoid_g
    hidden = (activated * up_pre).astype(jnp.bfloat16)
    part_out = jnp.dot(hidden, down_w, preferred_element_type=jnp.float32).astype(jnp.bfloat16)
    part_out, hidden, gate_pre, up_pre, c_first = lax.optimization_barrier(
        (part_out, hidden, gate_pre, up_pre, c_first)
    )
    sigmoid_g = jax.nn.sigmoid(gate_pre)
    activated = gate_pre * sigmoid_g
    out_first = reduce_first(part_out, groups)
    rows_c = swap_halves_second(c_along, c_first, groups)
    rows_c, out_first = lax.optimization_barrier((rows_c, out_first))
    out_parts = reduce_second(part_out, out_first, groups)
    grad_hidden = contract_last(rows_c, down_w)
    grad_upin = (grad_hidden * activated).astype(jnp.bfloat16)
    grad_gatein = (grad_hidden * up_pre * sigmoid_g * (1.0 + gate_pre * (1.0 - sigmoid_g))).astype(
        jnp.bfloat16
    )
    part_dx = (contract_last(grad_gatein, gate_w) + contract_last(grad_upin, up_w)).astype(
        jnp.bfloat16
    )
    part_dx, grad_upin, grad_gatein, out_parts = lax.optimization_barrier(
        (part_dx, grad_upin, grad_gatein, out_parts)
    )
    out_rows = along_expert(add_parts(out_parts)).astype(jnp.float32)
    new_gate = contract_first(rows_x, grad_gatein).astype(jnp.bfloat16)[None]
    new_up = contract_first(rows_x, grad_upin).astype(jnp.bfloat16)[None]
    new_down = contract_first(hidden, rows_c).astype(jnp.bfloat16)[None]
    dx_home, new_gate, new_up, new_down = lax.optimization_barrier(
        (reduce_dp(part_dx, groups), new_gate, new_up, new_down)
    )
    dx_rows = along_expert(dx_home)
    layer_out = jnp.dot(
        owner.astype(jnp.float32) * prob_rows[None, :],
        out_rows,
        precision=lax.Precision.HIGHEST,
        preferred_element_type=jnp.float32,
    ).astype(jnp.bfloat16)
    grad_tokens = jnp.dot(owner, dx_rows, preferred_element_type=jnp.float32).astype(jnp.bfloat16)
    score_rows = jnp.sum(rows_dy.astype(jnp.float32) * out_rows, axis=1)
    grad_probs = jnp.sum(jnp.where(chosen, score_rows[None, :], 0.0), axis=1).reshape(tok_count, top_k)
    return (layer_out, grad_tokens, grad_probs, new_gate, new_up, new_down)


def solution(mesh):
    return jax.shard_map(
        on_device,
        mesh=mesh,
        in_specs=(
            P(("dp", "expert"), None),
            P(("dp", "expert"), None),
            P(("dp", "expert"), None),
            P(("dp", "expert"), None),
            P("expert", None, "dp"),
            P("expert", None, "dp"),
            P("expert", "dp", None),
        ),
        out_specs=(
            P(("dp", "expert"), None),
            P(("dp", "expert"), None),
            P(("dp", "expert"), None),
            P("expert", None, "dp"),
            P("expert", None, "dp"),
            P("expert", "dp", None),
        ),
        check_vma=False,
    )
```

```python
import jax
import jax.numpy as jnp
from jax import lax
from jax.sharding import PartitionSpec as P


def slot_selection(flat_ids, experts, capacity):
    matches = (flat_ids[:, None] == jnp.arange(experts, dtype=jnp.int32)[None, :]).astype(jnp.int32)
    earlier = jnp.cumsum(matches, axis=0) - matches
    slot_pos = jnp.sum(earlier * matches, axis=1)
    target = jnp.where(flat_ids < experts, flat_ids * capacity + slot_pos, -1)
    return target[:, None] == jnp.arange(experts * capacity, dtype=jnp.int32)[None, :]


def contract_last(left, right):
    return lax.dot_general(
        left, right, (((1,), (1,)), ((), ())), preferred_element_type=jnp.float32
    )


def contract_first(left, right):
    return lax.dot_general(
        left, right, (((0,), (0,)), ((), ())), preferred_element_type=jnp.float32
    )


def along_expert(send_rows):
    return lax.all_to_all(send_rows, "expert", split_axis=0, concat_axis=0, tiled=True)


def pairs(groups, bit):
    return [(g, g ^ bit) for g in range(groups)]


def swap_halves_first(rows, groups):
    if groups != 4:
        return ()
    half = rows.shape[0] // 2
    return tuple(
        lax.ppermute(part, "dp", perm=pairs(groups, bit))
        for bit in (1, 2)
        for part in (rows[:half], rows[half:])
    )


def swap_halves_second(rows, first, groups):
    if groups != 4:
        return lax.all_gather(rows, "dp", axis=0, tiled=True)
    x_lo, x_hi, y_lo, y_hi = first
    diag_lo = lax.ppermute(x_lo, "dp", perm=pairs(groups, 2))
    diag_hi = lax.ppermute(y_hi, "dp", perm=pairs(groups, 1))
    return jnp.concatenate([rows, x_lo, x_hi, y_lo, y_hi, diag_lo, diag_hi], axis=0)


def replicate_dp(rows, groups):
    return swap_halves_second(rows, swap_halves_first(rows, groups), groups)


def reduce_first(partial_rows, groups):
    if groups != 4:
        return ()
    if isinstance(partial_rows, tuple):
        diag_lo, diag_hi = partial_rows[1:]
    else:
        to_diag = jnp.split(partial_rows, 4, axis=0)[3]
        half = to_diag.shape[0] // 2
        diag_lo, diag_hi = to_diag[:half], to_diag[half:]
    return (
        lax.ppermute(diag_lo, "dp", perm=pairs(groups, 1)),
        lax.ppermute(diag_hi, "dp", perm=pairs(groups, 2)),
    )


def reduce_second(partial_rows, first, groups):
    if groups != 4:
        return lax.psum_scatter(partial_rows, "dp", scatter_dimension=0, tiled=True)
    if isinstance(partial_rows, tuple):
        own, to_x, to_y = jnp.split(partial_rows[0], 3, axis=0)
    else:
        own, to_x, to_y, _ = jnp.split(partial_rows, 4, axis=0)
    via_x, via_y = first
    half = own.shape[0] // 2
    to_y = jnp.concatenate(
        [(to_y[:half].astype(jnp.float32) + via_x.astype(jnp.float32)).astype(jnp.bfloat16), to_y[half:]], 0
    )
    to_x = jnp.concatenate(
        [to_x[:half], (to_x[half:].astype(jnp.float32) + via_y.astype(jnp.float32)).astype(jnp.bfloat16)], 0
    )
    from_x = lax.ppermute(to_x, "dp", perm=pairs(groups, 1))
    from_y = lax.ppermute(to_y, "dp", perm=pairs(groups, 2))
    return own, from_x, from_y


def add_parts(parts):
    if not isinstance(parts, tuple):
        return parts
    own, from_x, from_y = parts
    total = own.astype(jnp.float32) + from_x.astype(jnp.float32) + from_y.astype(jnp.float32)
    return total.astype(jnp.bfloat16)


def reduce_dp(partial_rows, groups):
    return add_parts(reduce_second(partial_rows, reduce_first(partial_rows, groups), groups))


def gather_back(partial_rows, groups):
    summed = reduce_dp(partial_rows, groups)
    return lax.all_to_all(summed, "expert", split_axis=0, concat_axis=0, tiled=True)


def on_device(tokens, gate_probs, expert_ids, cotangent, w_gate, w_up, w_down):
    tok_count, model_width = tokens.shape
    top_k = expert_ids.shape[1]
    experts = lax.axis_size("expert")
    groups = lax.axis_size("dp")
    capacity = 3 * tok_count * top_k // (16 * experts)
    chosen = slot_selection(expert_ids.reshape(-1), experts, capacity)
    owner = jnp.any(chosen.reshape(tok_count, top_k, -1), axis=1).astype(jnp.bfloat16)
    send_x = contract_first(owner, tokens).astype(jnp.bfloat16)
    rows_dy = contract_first(owner, cotangent).astype(jnp.bfloat16)
    prob_rows = jnp.sum(jnp.where(chosen, gate_probs.reshape(-1)[:, None], 0.0), axis=0)
    send_c = (prob_rows[:, None] * rows_dy.astype(jnp.float32)).astype(jnp.bfloat16)
    rows_x = replicate_dp(along_expert(send_x), groups)
    rows_x, c_along = lax.optimization_barrier((rows_x, along_expert(send_c)))
    c_first = swap_halves_first(c_along, groups)
    gate_w = w_gate[0]
    up_w = w_up[0]
    down_w = w_down[0]
    gate_pre = jnp.dot(rows_x, gate_w, preferred_element_type=jnp.float32)
    up_pre = jnp.dot(rows_x, up_w, preferred_element_type=jnp.float32)
    sigmoid_g = jax.nn.sigmoid(gate_pre)
    activated = gate_pre * sigmoid_g
    hidden = (activated * up_pre).astype(jnp.bfloat16)
    def output_part(lo, hi):
        return jnp.dot(hidden[lo:hi], down_w, preferred_element_type=jnp.float32).astype(jnp.bfloat16)

    rows = hidden.shape[0]
    if groups == 4:
        block = rows // 4
        part_out = (
            output_part(0, 3 * block),
            output_part(3 * block, 3 * block + block // 2),
            output_part(3 * block + block // 2, rows),
        )
    else:
        part_out = output_part(0, rows)
    part_out, hidden, gate_pre, up_pre, c_first = lax.optimization_barrier(
        (part_out, hidden, gate_pre, up_pre, c_first)
    )
    sigmoid_g = jax.nn.sigmoid(gate_pre)
    activated = gate_pre * sigmoid_g
    out_first = reduce_first(part_out, groups)
    rows_c = swap_halves_second(c_along, c_first, groups)
    rows_c, out_first = lax.optimization_barrier((rows_c, out_first))
    out_parts = reduce_second(part_out, out_first, groups)
    grad_hidden = contract_last(rows_c, down_w)
    grad_upin = (grad_hidden * activated).astype(jnp.bfloat16)
    grad_gatein = (grad_hidden * up_pre * sigmoid_g * (1.0 + gate_pre * (1.0 - sigmoid_g))).astype(
        jnp.bfloat16
    )
    part_dx = (contract_last(grad_gatein, gate_w) + contract_last(grad_upin, up_w)).astype(
        jnp.bfloat16
    )
    part_dx, grad_upin, grad_gatein, out_parts = lax.optimization_barrier(
        (part_dx, grad_upin, grad_gatein, out_parts)
    )
    out_rows = along_expert(add_parts(out_parts)).astype(jnp.float32)
    new_gate = contract_first(rows_x, grad_gatein).astype(jnp.bfloat16)[None]
    new_up = contract_first(rows_x, grad_upin).astype(jnp.bfloat16)[None]
    new_down = contract_first(hidden, rows_c).astype(jnp.bfloat16)[None]
    dx_home, new_gate, new_up, new_down = lax.optimization_barrier(
        (reduce_dp(part_dx, groups), new_gate, new_up, new_down)
    )
    dx_rows = along_expert(dx_home)
    layer_out = jnp.dot(
        owner.astype(jnp.float32) * prob_rows[None, :],
        out_rows,
        precision=lax.Precision.HIGHEST,
        preferred_element_type=jnp.float32,
    ).astype(jnp.bfloat16)
    grad_tokens = jnp.dot(owner, dx_rows, preferred_element_type=jnp.float32).astype(jnp.bfloat16)
    score_rows = jnp.sum(rows_dy.astype(jnp.float32) * out_rows, axis=1)
    grad_probs = jnp.sum(jnp.where(chosen, score_rows[None, :], 0.0), axis=1).reshape(tok_count, top_k)
    return (layer_out, grad_tokens, grad_probs, new_gate, new_up, new_down)


def solution(mesh):
    return jax.shard_map(
        on_device,
        mesh=mesh,
        in_specs=(
            P(("dp", "expert"), None),
            P(("dp", "expert"), None),
            P(("dp", "expert"), None),
            P(("dp", "expert"), None),
            P("expert", None, "dp"),
            P("expert", None, "dp"),
            P("expert", "dp", None),
        ),
        out_specs=(
            P(("dp", "expert"), None),
            P(("dp", "expert"), None),
            P(("dp", "expert"), None),
            P("expert", None, "dp"),
            P("expert", None, "dp"),
            P("expert", "dp", None),
        ),
        check_vma=False,
    )
```
